128 devices in a mesh: seq: 16 (over y, x), expert: 4 (over z), mp: 2 (over core).
Axes of the slice: x: 4, y: 4, z: 4, core: 2. Of those that a mesh axis runs over, the one named last changes fastest.
Arguments:
- activations: bfloat16 [16384, 4096], P('seq', ('expert', 'mp')), may hold values from -6 to 6
- output_gradient: bfloat16 [16384, 4096], P('seq', ('expert', 'mp')), may hold values from -1.5 to 1.5
- input_state_map: bfloat16 [16384, 16], P('seq'), may hold values from -3 to 3
- output_state_map: bfloat16 [16384, 16], P('seq'), may hold values from -3 to 3
- head_decay_speed: float32 [64], P(('expert', 'mp')), may hold values from 3.0517578e-06 to 0.05, as said below
- spike_decay_level: int32 [16384], P('seq'), may hold values from 0 to 2, as said below
- assign: int32 [128], replicated, may hold values from 0 to 15, as said below
- expert_up_weight: bfloat16 [4, 4096, 12288], P('expert', 'mp', 'seq'), may hold values from -0.09375 to 0.09375
- expert_down_weight: bfloat16 [4, 12288, 4096], P('expert', 'seq', 'mp'), may hold values from -0.0546875 to 0.0546875
Outputs:
- grad_x: float32 [16384, 4096], P('seq', ('expert', 'mp'))
- grad_w_up: float32 [4, 4096, 12288], P('expert', 'mp', 'seq')
- grad_w_down: float32 [4, 12288, 4096], P('expert', 'seq', 'mp')
The draws below stay inside these ranges and needn't reach their ends.
Inputs may be any that keep to these rules, and one draw needn't show every extreme that they name: `head_decay_speed`: some of the heads keep a tenth or more of their state over the whole sequence, the others lose it within some tens of tokens. `spike_decay_level`: at most three tokens of the sequence have a nonzero level. `assign`: numbers below 4 are the window's experts: the 8 blocks of one index of seq hold at most one block of each of them, each takes at most 8 blocks in all, and one takes exactly 8.
All inputs are finite; a program needn't handle non-finite values.
Results may differ from the reference program's by a relative error of at most 0.019.
Values may be sent and summed in bfloat16 or wider, within the bound.
No kernel may reach another device: no remote copies, remote signals or barrier semaphores. Data moves between devices by JAX's collectives and lax.ppermute only.
A program may use at most 128 MiB of HBM per device.

```python
import math
import jax
import jax.numpy as jnp
from jax import lax

D = 4096
FF = 12288
HEAD = 64
STATE = 16
BLOCK = 128
EXP_ALL = 16
SEQUENCE_TOKENS = 16384
HEADS = 64
EXPERTS = 4
BLOCKS_DEV = 8
SEQ_BLOCKS = 128
SLOTS = 8
N_SEQ = 16
N_MP = 2


def draw_head_decay_speed(key, part):
    key_slow, key_fast, key_pick = jax.random.split(key, 3)
    slow_rate = jax.random.uniform(key_slow, (HEADS,), jnp.float32, math.log(0.05 / SEQUENCE_TOKENS), math.log(0.5 / SEQUENCE_TOKENS))
    fast_rate = jax.random.uniform(key_fast, (HEADS,), jnp.float32, math.log(0.02), math.log(0.05))
    keeping = jax.random.uniform(key_pick, (HEADS,), jnp.float32) < 0.5
    return jnp.exp(jnp.where(keeping, slow_rate, fast_rate)).astype(jnp.float32)


def draw_spike_decay_level(key, part):
    position_random_key, level_random_key = jax.random.split(key, 2)
    spike_positions = jax.random.randint(position_random_key, (3,), 0, SEQUENCE_TOKENS)
    spike_level_list = jax.random.randint(level_random_key, (3,), 1, 3).at[0].set(2)
    return jnp.zeros((SEQUENCE_TOKENS,), jnp.int32).at[spike_positions].max(spike_level_list.astype(jnp.int32))


def draw_assign(key, part):
    key_list = jax.random.split(key, 4)
    route_table = jax.random.randint(key_list[0], (N_SEQ, BLOCKS_DEV), EXPERTS, EXP_ALL).astype(jnp.int32)
    ranking = jax.random.permutation(key_list[1], EXPERTS)
    block_places = jax.vmap(lambda sub_key: jax.random.permutation(sub_key, BLOCKS_DEV))(jax.random.split(key_list[2], N_SEQ))
    shard_keys = jax.random.split(key_list[3], EXPERTS)
    for expert in range(EXPERTS):
        rank_now = jnp.minimum(ranking[expert], 2)
        expert_load = jnp.maximum(1, jnp.right_shift(SLOTS, rank_now))
        shuffled = jax.random.permutation(shard_keys[expert], N_SEQ)
        place_of = jnp.argsort(shuffled)
        is_taken = place_of < expert_load
        marked = is_taken[:, None] & (jnp.arange(BLOCKS_DEV)[None, :] == block_places[:, expert][:, None])
        route_table = jnp.where(marked, expert, route_table)
    return route_table.reshape(SEQ_BLOCKS).astype(jnp.int32)


def shard_levels(rng, shape, cuts, low, top_value):
    level = 1.0
    for dim, blocks in cuts:
        steps = jax.random.uniform(jax.random.fold_in(jax.random.fold_in(rng, 6), dim), (blocks,), jnp.float32, low / len(cuts), top_value / len(cuts))
        level = level * jnp.repeat(jnp.exp(steps), shape[dim] // blocks).reshape((-1,) + (1,) * (len(shape) - 1 - dim))
    return level


def gaussian(rng, shape, deviation, most, pieces=(), held_as=jnp.bfloat16):
    array = jax.random.normal(rng, shape, jnp.float32) * deviation
    if len(pieces) > 0:
        array = shard_levels(rng, shape, pieces, -0.22, 0.18) * array
    return jnp.clip(array, min=-most, max=most).astype(held_as)


def setup_inputs(seed: int = 0) -> dict:
    streams_of = jax.random.split(jax.random.key(seed), 10)
    activations = gaussian(streams_of[0], (SEQUENCE_TOKENS, D), 1.0, 6.0, ((0, 16), (1, 8)))
    output_gradient = gaussian(streams_of[1], (SEQUENCE_TOKENS, D), 0.25, 1.5, ((0, 16), (1, 8)))
    input_state_map = gaussian(streams_of[2], (SEQUENCE_TOKENS, STATE), 0.5, 3.0, ((0, 16),))
    output_state_map = gaussian(streams_of[3], (SEQUENCE_TOKENS, STATE), 0.5, 3.0, ((0, 16),))
    head_decay_speed = draw_head_decay_speed(jax.random.fold_in(streams_of[9], 71), 0)
    spike_decay_level = draw_spike_decay_level(jax.random.fold_in(streams_of[9], 71), 0)
    assign = draw_assign(jax.random.fold_in(streams_of[9], 71), 0)
    expert_up_weight = gaussian(streams_of[7], (EXPERTS, D, FF), D ** -0.5, 0.09375, ((0, 4), (1, 2), (2, 16)))
    expert_down_weight = gaussian(streams_of[8], (EXPERTS, FF, D), FF ** -0.5, 0.0546875, ((0, 4), (1, 16), (2, 2)))
    return dict(activations=activations, output_gradient=output_gradient, input_state_map=input_state_map, output_state_map=output_state_map, head_decay_speed=head_decay_speed, spike_decay_level=spike_decay_level, assign=assign, expert_up_weight=expert_up_weight, expert_down_weight=expert_down_weight)


spike_position_step = 0.3
highest = lax.Precision.HIGHEST

def rounded(rounded_in):
    return lax.optimization_barrier(rounded_in.astype(jnp.bfloat16)).astype(jnp.float32)

def slot_rows(chosen, present, select, blocks):
    position = jnp.argmax(chosen.astype(jnp.int32), axis=1).astype(jnp.int32)
    picked = blocks[jnp.arange(N_SEQ), position].astype(jnp.float32)
    picked = picked * present.astype(jnp.float32)[:, None, None]
    slot_block = jnp.einsum('js,srd->jrd', select, picked, precision=highest)
    return slot_block.astype(jnp.bfloat16).reshape(SLOTS * BLOCK, D)

def reference(activations, output_gradient, input_state_map, output_state_map, head_decay_speed, spike_decay_level, assign, expert_up_weight, expert_down_weight):
    input_scale = jnp.sqrt(1.0 - jnp.exp(-2.0 * head_decay_speed))
    every_spike_level = -head_decay_speed[None, :] - spike_position_step * spike_decay_level.astype(jnp.float32)[:, None]
    factor_all = jnp.exp(every_spike_level)
    b_float = input_state_map.astype(jnp.float32)
    c_float = output_state_map.astype(jnp.float32)
    scaled = activations.astype(jnp.float32).reshape(SEQUENCE_TOKENS, HEADS, HEAD) * input_scale[None, :, None]

    def forward_step(scan_state, step_in):
        decay_factor, x_now, b_now, c_now = step_in
        scan_state = decay_factor[:, None, None] * scan_state + x_now[:, :, None] * b_now[None, None, :]
        return (scan_state, jnp.einsum('hpn,n->hp', scan_state, c_now, precision=highest))
    _, outputs = lax.scan(forward_step, jnp.zeros((HEADS, HEAD, STATE), jnp.float32), (factor_all, scaled, b_float, c_float))
    mixed_out = (activations.astype(jnp.float32) + outputs.reshape(SEQUENCE_TOKENS, D)).astype(jnp.bfloat16)
    route_table = assign.reshape(N_SEQ, BLOCKS_DEV)
    mixed_blocks = mixed_out.reshape(N_SEQ, BLOCKS_DEV, BLOCK, D)
    grad_blocks = output_gradient.reshape(N_SEQ, BLOCKS_DEV, BLOCK, D)
    half_width = D // N_MP
    group_width = FF // N_SEQ
    token_grad = jnp.zeros((N_SEQ, BLOCKS_DEV, BLOCK, D), jnp.float32)
    up_grads = []
    down_grads = []
    for expert in range(EXPERTS):
        chosen = route_table == expert
        present = jnp.any(chosen, axis=1)
        slot_of = jnp.cumsum(present.astype(jnp.int32)) - 1
        select = ((slot_of[None, :] == jnp.arange(SLOTS)[:, None]) & present[None, :]).astype(jnp.float32)
        x_rows = slot_rows(chosen, present, select, mixed_blocks)
        g_rows = slot_rows(chosen, present, select, grad_blocks)
        up_w = expert_up_weight[expert]
        down_w = expert_down_weight[expert]
        pre_act = jnp.zeros((SLOTS * BLOCK, FF), jnp.float32)
        act_grad = jnp.zeros((SLOTS * BLOCK, FF), jnp.float32)
        for part_index in range(N_MP):
            low_index = part_index * half_width
            pre_act = pre_act + rounded(jnp.dot(x_rows[:, low_index:low_index + half_width], up_w[low_index:low_index + half_width], preferred_element_type=jnp.float32))
            act_grad = act_grad + rounded(jnp.dot(g_rows[:, low_index:low_index + half_width], down_w[:, low_index:low_index + half_width].T, preferred_element_type=jnp.float32))
        activation = jax.nn.silu(pre_act).astype(jnp.bfloat16)
        down_grads.append(jnp.dot(activation.T, g_rows, preferred_element_type=jnp.float32))
        sigmoid_pre = jax.nn.sigmoid(pre_act)
        pre_grad = (act_grad * sigmoid_pre * (1.0 + pre_act * (1.0 - sigmoid_pre))).astype(jnp.bfloat16)
        up_grads.append(jnp.dot(x_rows.T, pre_grad, preferred_element_type=jnp.float32))
        row_grad = jnp.zeros((SLOTS * BLOCK, D), jnp.float32)
        for group_index in range(N_SEQ):
            low_index = group_index * group_width
            row_grad = row_grad + rounded(jnp.dot(pre_grad[:, low_index:low_index + group_width], up_w[:, low_index:low_index + group_width].T, preferred_element_type=jnp.float32))
        row_grad = row_grad.astype(jnp.bfloat16).astype(jnp.float32).reshape(SLOTS, BLOCK, D)
        back_rows = jnp.einsum('js,jrd->srd', select, row_grad, precision=highest)
        token_grad = token_grad + chosen.astype(jnp.float32)[:, :, None, None] * back_rows[:, None]
    total_grad = output_gradient.astype(jnp.float32) + token_grad.reshape(SEQUENCE_TOKENS, D)
    grad_view = total_grad.reshape(SEQUENCE_TOKENS, HEADS, HEAD)

    def backward_step(carry, step_in):
        adjoint, factor_next = carry
        decay_factor, grad_now, b_now, c_now = step_in
        adjoint = factor_next[:, None, None] * adjoint + grad_now[:, :, None] * c_now[None, None, :]
        return ((adjoint, decay_factor), jnp.einsum('hpn,n->hp', adjoint, b_now, precision=highest))
    start_carry = (jnp.zeros((HEADS, HEAD, STATE), jnp.float32), jnp.ones((HEADS,), jnp.float32))
    _, scan_grad = lax.scan(backward_step, start_carry, (factor_all, grad_view, b_float, c_float), reverse=True)
    grad_x = total_grad + (input_scale[None, :, None] * scan_grad).reshape(SEQUENCE_TOKENS, D)
    return (grad_x, jnp.stack(up_grads), jnp.stack(down_grads))
```

```python
import jax
import jax.numpy as jnp
from jax import lax
from jax.sharding import PartitionSpec as P

HEAD = 64
STATE = 16
BLOCK = 128


spike_position_step = 0.3
highest = lax.Precision.HIGHEST


def carried_sum(values_all, level_all, own, earlier):
    count = level_all.shape[0]
    ids = jnp.arange(count)
    j, k = ids[:, None], ids[None, :]
    if earlier:
        between = (j < k) & (k < own)
        valid = ids < own
    else:
        between = (own < k) & (k < j)
        valid = ids > own
    exponent = jnp.sum(jnp.where(between[:, :, None], level_all[None], 0.0), axis=1)
    weight = jnp.where(valid[:, None], jnp.exp(exponent), 0.0)
    return jnp.sum(weight[:, :, None] * values_all.astype(jnp.float32), axis=0)


def mp_sum(part):
    part = part.astype(jnp.bfloat16)
    count = lax.axis_size("mp")
    total = part.astype(jnp.float32)
    for shift in range(1, count):
        pairs = [(src, (src + shift) % count) for src in range(count)]
        total = total + lax.ppermute(part, "mp", pairs).astype(jnp.float32)
    return total


def dispatch_pairs(exp_count, mp_count, shift):
    return [
        (src, ((src % exp_count + shift) % exp_count) * mp_count + src // exp_count)
        for src in range(exp_count * mp_count)
    ]


def dispatch(picks, exp_index, exp_count, mp_count, my_slice):
    position = my_slice % exp_count
    received = []
    for shift in range(exp_count):
        send = lax.dynamic_index_in_dim(picks, (position + shift) % exp_count, 0, keepdims=False)
        pairs = dispatch_pairs(exp_count, mp_count, shift)
        received.append(lax.ppermute(send, ("expert", "mp"), pairs))
    received = jnp.stack(received)
    order = (exp_index - jnp.arange(exp_count)) % exp_count
    placed = jnp.take(received, order, axis=0)
    rows, width = placed.shape[1], placed.shape[2]
    return placed.transpose(1, 0, 2).reshape(rows, exp_count * width)


def give_back(rows_half, exp_index, exp_count, mp_count):
    width = rows_half.shape[1] // exp_count
    pieces = rows_half.reshape(rows_half.shape[0], exp_count, width)
    received = []
    for shift in range(exp_count):
        column = (exp_index - shift) % exp_count
        send = lax.dynamic_index_in_dim(pieces, column, 1, keepdims=False)
        pairs = [(dst, src) for src, dst in dispatch_pairs(exp_count, mp_count, shift)]
        received.append(lax.ppermute(send, ("expert", "mp"), pairs))
    return jnp.stack(received)


def rounded(rounded_in):
    return lax.optimization_barrier(rounded_in.astype(jnp.bfloat16)).astype(jnp.float32)


def split_parts(values):
    high_part = values.astype(jnp.bfloat16)
    low_part = (values - high_part.astype(jnp.float32)).astype(jnp.bfloat16)
    return (high_part, low_part)


def mixing(cum_block, scores, causal):
    spread = cum_block.T[:, :, None] - cum_block.T[:, None, :]
    spread = jnp.where(causal[None], spread, -jnp.inf)
    return jnp.exp(spread) * scores[None]


def compact(select, gathered, half_width):
    shaped = gathered.reshape(select.shape[1], -1, half_width)
    rows_out = jnp.einsum("js,srf->jrf", select, shaped, preferred_element_type=jnp.float32)
    return rows_out.astype(jnp.bfloat16).reshape(-1, half_width)


def per_device(
    activations,
    output_gradient,
    input_state_map,
    output_state_map,
    head_decay_speed,
    spike_decay_level,
    assign,
    expert_up_weight,
    expert_down_weight,
):
    tokens, slice_width = activations.shape
    heads_dev = slice_width // HEAD
    seq_count = lax.axis_size("seq")
    exp_count = lax.axis_size("expert")
    mp_count = lax.axis_size("mp")
    seq_index = lax.axis_index("seq")
    exp_index = lax.axis_index("expert")
    mp_index = lax.axis_index("mp")
    my_slice = exp_index * mp_count + mp_index
    half_width = slice_width * exp_count
    slot_total = seq_count // 2
    input_scale = jnp.sqrt(1.0 - jnp.exp(-2.0 * head_decay_speed))
    cum_level = jnp.cumsum(
        -head_decay_speed[None, :]
        - spike_position_step * spike_decay_level.astype(jnp.float32)[:, None],
        axis=0,
    )
    b_float = input_state_map.astype(jnp.float32)
    c_float = output_state_map.astype(jnp.float32)
    act_heads = activations.reshape(tokens, heads_dev, HEAD)
    scaled = act_heads.astype(jnp.float32) * input_scale[None, :, None]
    span_rows = min(512, tokens)
    span_count = tokens // span_rows
    causal = jnp.arange(span_rows)[:, None] >= jnp.arange(span_rows)[None, :]
    zero_level = jnp.zeros((heads_dev,), jnp.float32)
    carry_state = jnp.zeros((heads_dev, HEAD, STATE), jnp.float32)
    pieces = []
    for position in range(span_count):
        first_row = position * span_rows
        last_row = first_row + span_rows
        cum_block = cum_level[first_row:last_row]
        start_level = cum_level[first_row - 1] if position > 0 else zero_level
        scores = jnp.dot(
            output_state_map[first_row:last_row],
            input_state_map[first_row:last_row].T,
            preferred_element_type=jnp.float32,
        )
        weights = mixing(cum_block, scores, causal)
        weight_high, weight_low = split_parts(weights)
        x_span = act_heads[first_row:last_row]
        inner_part = jnp.einsum(
            "hts,shp->thp", weight_high, x_span, preferred_element_type=jnp.float32
        )
        inner_part = inner_part + jnp.einsum(
            "hts,shp->thp", weight_low, x_span, preferred_element_type=jnp.float32
        )
        inner_part = inner_part * input_scale[None, :, None]
        carried = jnp.exp(cum_block - start_level[None, :])[:, :, None] * jnp.einsum(
            "tn,hpn->thp", c_float[first_row:last_row], carry_state, precision=highest
        )
        pieces.append(inner_part + carried)
        end_level = cum_block[-1]
        tail_decay = jnp.exp(end_level[None, :] - cum_block)
        carry_state = jnp.exp(end_level - start_level)[:, None, None] * carry_state + jnp.einsum(
            "shp,sn->hpn",
            scaled[first_row:last_row] * tail_decay[:, :, None],
            b_float[first_row:last_row],
            precision=highest,
        )
    flat_state = carry_state.reshape(heads_dev, HEAD * STATE)
    level_all = lax.all_gather(cum_level[-1], "seq")
    state_all = lax.all_gather(flat_state.astype(jnp.bfloat16), "seq")
    incoming = carried_sum(state_all, level_all, seq_index, True)
    incoming = incoming.reshape(heads_dev, HEAD, STATE)
    outputs = jnp.concatenate(pieces, axis=0) + jnp.exp(cum_level)[:, :, None] * jnp.einsum(
        "tn,hpn->thp", c_float, incoming, precision=highest
    )
    mixed_out = (activations.astype(jnp.float32) + outputs.reshape(tokens, slice_width)).astype(
        jnp.bfloat16
    )
    blocks_dev = tokens // BLOCK
    route_table = assign.reshape(seq_count, blocks_dev)
    own_row = lax.dynamic_index_in_dim(route_table, seq_index, 0, keepdims=False)
    chosen = (own_row[None, :] == jnp.arange(exp_count)[:, None]).astype(jnp.bfloat16)
    h_pick = jnp.einsum(
        "eb,brf->erf",
        chosen,
        mixed_out.reshape(blocks_dev, BLOCK, slice_width),
        preferred_element_type=jnp.float32,
    ).astype(jnp.bfloat16)
    g_pick = jnp.einsum(
        "eb,brf->erf",
        chosen,
        output_gradient.reshape(blocks_dev, BLOCK, slice_width),
        preferred_element_type=jnp.float32,
    ).astype(jnp.bfloat16)
    h_block = dispatch(h_pick, exp_index, exp_count, mp_count, my_slice)
    g_block = dispatch(g_pick, exp_index, exp_count, mp_count, my_slice)
    h_all, g_all = (
        lax.all_gather(h_block, "seq", axis=0, tiled=True),
        lax.all_gather(g_block, "seq", axis=0, tiled=True),
    )
    present = jnp.any(route_table == exp_index, axis=1)
    slot_of = jnp.cumsum(present.astype(jnp.int32)) - 1
    select = ((slot_of[None, :] == jnp.arange(slot_total)[:, None]) & present[None, :]).astype(
        jnp.bfloat16
    )
    x_rows = compact(select, h_all, half_width)
    g_rows = compact(select, g_all, half_width)
    up_local = expert_up_weight[0]
    down_local = expert_down_weight[0]
    pre_act = mp_sum(jnp.dot(x_rows, up_local, preferred_element_type=jnp.float32))
    activation = jax.nn.silu(pre_act).astype(jnp.bfloat16)
    down_grad = jnp.einsum("tf,td->fd", activation, g_rows, preferred_element_type=jnp.float32)
    act_grad = mp_sum(
        jnp.einsum("td,fd->tf", g_rows, down_local, preferred_element_type=jnp.float32)
    )
    sigmoid_pre = jax.nn.sigmoid(pre_act)
    pre_grad = (act_grad * sigmoid_pre * (1.0 + pre_act * (1.0 - sigmoid_pre))).astype(jnp.bfloat16)
    up_grad = jnp.einsum("td,tf->df", x_rows, pre_grad, preferred_element_type=jnp.float32)
    row_grad = jnp.einsum("tf,df->td", pre_grad, up_local, preferred_element_type=jnp.float32)
    row_grad = row_grad.astype(jnp.bfloat16).reshape(slot_total, BLOCK, half_width)
    spread_rows = jnp.einsum("js,jrf->srf", select, row_grad, preferred_element_type=jnp.float32)
    back_rows = lax.psum_scatter(
        spread_rows.reshape(BLOCK * lax.axis_size("seq"), half_width).astype(jnp.bfloat16),
        "seq",
        scatter_dimension=0,
        tiled=True,
    )
    returned = give_back(back_rows, exp_index, exp_count, mp_count)
    position = my_slice % exp_count
    chosen_by_shift = jnp.take(chosen, (position + jnp.arange(exp_count)) % exp_count, axis=0)
    token_grad = jnp.einsum(
        "kb,krf->brf", chosen_by_shift, returned, preferred_element_type=jnp.float32
    )
    total_grad = output_gradient.astype(jnp.float32) + token_grad.reshape(tokens, slice_width)
    grad_view = total_grad.reshape(tokens, heads_dev, HEAD)
    adjoint = jnp.zeros((heads_dev, HEAD, STATE), jnp.float32)
    back_pieces = [None] * span_count
    for position in reversed(range(span_count)):
        first_row = position * span_rows
        last_row = first_row + span_rows
        cum_block = cum_level[first_row:last_row]
        start_level = cum_level[first_row - 1] if position > 0 else zero_level
        scores = jnp.dot(
            output_state_map[first_row:last_row],
            input_state_map[first_row:last_row].T,
            preferred_element_type=jnp.float32,
        )
        weights = mixing(cum_block, scores, causal)
        weight_high, weight_low = split_parts(weights)
        grad_high, grad_low = split_parts(grad_view[first_row:last_row])
        inner_part = jnp.einsum(
            "hts,thp->shp", weight_high, grad_high, preferred_element_type=jnp.float32
        )
        inner_part = inner_part + jnp.einsum(
            "hts,thp->shp", weight_high, grad_low, preferred_element_type=jnp.float32
        )
        inner_part = inner_part + jnp.einsum(
            "hts,thp->shp", weight_low, grad_high, preferred_element_type=jnp.float32
        )
        end_level = cum_block[-1]
        tail_decay = jnp.exp(end_level[None, :] - cum_block)
        carried = tail_decay[:, :, None] * jnp.einsum(
            "sn,hpn->shp", b_float[first_row:last_row], adjoint, precision=highest
        )
        back_pieces[position] = inner_part + carried
        lead_decay = jnp.exp(cum_block - start_level[None, :])
        adjoint = jnp.exp(end_level - start_level)[:, None, None] * adjoint + jnp.einsum(
            "rhp,rn->hpn",
            grad_view[first_row:last_row] * lead_decay[:, :, None],
            c_float[first_row:last_row],
            precision=highest,
        )
    flat_adjoint = adjoint.reshape(heads_dev, HEAD * STATE)
    adjoint_all = lax.all_gather(flat_adjoint.astype(jnp.bfloat16), "seq")
    later_adjoint = carried_sum(adjoint_all, level_all, seq_index, False)
    later_adjoint = later_adjoint.reshape(heads_dev, HEAD, STATE)
    scan_grad = jnp.concatenate(back_pieces, axis=0) + jnp.exp(cum_level[-1][None, :] - cum_level)[
        :, :, None
    ] * jnp.einsum("sn,hpn->shp", b_float, later_adjoint, precision=highest)
    grad_x = total_grad + (input_scale[None, :, None] * scan_grad).reshape(tokens, slice_width)
    return (grad_x, up_grad[None], down_grad[None])


def solution(mesh):
    in_specs = (
        P("seq", ("expert", "mp")),
        P("seq", ("expert", "mp")),
        P("seq", None),
        P("seq", None),
        P(("expert", "mp")),
        P("seq"),
        P(),
        P("expert", "mp", "seq"),
        P("expert", "seq", "mp"),
    )
    out_specs = (P("seq", ("expert", "mp")), P("expert", "mp", "seq"), P("expert", "seq", "mp"))
    return jax.shard_map(
        per_device, mesh=mesh, in_specs=in_specs, out_specs=out_specs, check_vma=False
    )
```

```python
import jax
import jax.numpy as jnp
from jax import lax
from jax.sharding import PartitionSpec as P

HEAD = 64
STATE = 16
BLOCK = 128


spike_position_step = 0.3
highest = lax.Precision.HIGHEST


def carried_sum(values_all, level_all, own, earlier):
    count = level_all.shape[0]
    ids = jnp.arange(count)
    j, k = ids[:, None], ids[None, :]
    if earlier:
        between = (j < k) & (k < own)
        valid = ids < own
    else:
        between = (own < k) & (k < j)
        valid = ids > own
    exponent = jnp.sum(jnp.where(between[:, :, None], level_all[None], 0.0), axis=1)
    weight = jnp.where(valid[:, None], jnp.exp(exponent), 0.0)
    return jnp.sum(weight[:, :, None] * values_all.astype(jnp.float32), axis=0)


def mp_sum(part):
    part = part.astype(jnp.bfloat16)
    count = lax.axis_size("mp")
    total = part.astype(jnp.float32)
    for shift in range(1, count):
        pairs = [(src, (src + shift) % count) for src in range(count)]
        total = total + lax.ppermute(part, "mp", pairs).astype(jnp.float32)
    return total


def dispatch_pairs(exp_count, mp_count, shift):
    return [
        (src, ((src % exp_count + shift) % exp_count) * mp_count + src // exp_count)
        for src in range(exp_count * mp_count)
    ]


def dispatch(picks, exp_index, exp_count, mp_count, my_slice):
    position = my_slice % exp_count
    received = []
    for shift in range(exp_count):
        send = lax.dynamic_index_in_dim(picks, (position + shift) % exp_count, 0, keepdims=False)
        pairs = dispatch_pairs(exp_count, mp_count, shift)
        received.append(lax.ppermute(send, ("expert", "mp"), pairs))
    received = jnp.stack(received)
    order = (exp_index - jnp.arange(exp_count)) % exp_count
    placed = jnp.take(received, order, axis=0)
    rows, width = placed.shape[1], placed.shape[2]
    return placed.transpose(1, 0, 2).reshape(rows, exp_count * width)


def give_back(rows_half, exp_index, exp_count, mp_count):
    width = rows_half.shape[1] // exp_count
    pieces = rows_half.reshape(rows_half.shape[0], exp_count, width)
    received = []
    for shift in range(exp_count):
        column = (exp_index - shift) % exp_count
        send = lax.dynamic_index_in_dim(pieces, column, 1, keepdims=False)
        pairs = [(dst, src) for src, dst in dispatch_pairs(exp_count, mp_count, shift)]
        received.append(lax.ppermute(send, ("expert", "mp"), pairs))
    return jnp.stack(received)


def rounded(rounded_in):
    return lax.optimization_barrier(rounded_in.astype(jnp.bfloat16)).astype(jnp.float32)


def split_parts(values):
    high_part = values.astype(jnp.bfloat16)
    low_part = (values - high_part.astype(jnp.float32)).astype(jnp.bfloat16)
    return (high_part, low_part)


def mixing(cum_block, scores, causal):
    spread = cum_block.T[:, :, None] - cum_block.T[:, None, :]
    spread = jnp.where(causal[None], spread, -jnp.inf)
    return jnp.exp(spread) * scores[None]


def compact(select, gathered, half_width):
    shaped = gathered.reshape(select.shape[1], -1, half_width)
    rows_out = jnp.einsum("js,srf->jrf", select, shaped, preferred_element_type=jnp.float32)
    return rows_out.astype(jnp.bfloat16).reshape(-1, half_width)


def per_device(
    activations,
    output_gradient,
    input_state_map,
    output_state_map,
    head_decay_speed,
    spike_decay_level,
    assign,
    expert_up_weight,
    expert_down_weight,
):
    tokens, slice_width = activations.shape
    heads_dev = slice_width // HEAD
    seq_count = lax.axis_size("seq")
    exp_count = lax.axis_size("expert")
    mp_count = lax.axis_size("mp")
    seq_index = lax.axis_index("seq")
    exp_index = lax.axis_index("expert")
    mp_index = lax.axis_index("mp")
    my_slice = exp_index * mp_count + mp_index
    half_width = slice_width * exp_count
    slot_total = seq_count // 2
    blocks_dev = tokens // BLOCK
    route_table = assign.reshape(seq_count, blocks_dev)
    own_row = lax.dynamic_index_in_dim(route_table, seq_index, 0, keepdims=False)
    chosen = (own_row[None, :] == jnp.arange(exp_count)[:, None]).astype(jnp.bfloat16)
    g_pick = jnp.einsum(
        "eb,brf->erf",
        chosen,
        output_gradient.reshape(blocks_dev, BLOCK, slice_width),
        preferred_element_type=jnp.float32,
    ).astype(jnp.bfloat16)
    g_block = dispatch(g_pick, exp_index, exp_count, mp_count, my_slice)
    g_all = lax.all_gather(g_block, "seq", axis=0, tiled=True)
    input_scale = jnp.sqrt(1.0 - jnp.exp(-2.0 * head_decay_speed))
    cum_level = jnp.cumsum(
        -head_decay_speed[None, :]
        - spike_position_step * spike_decay_level.astype(jnp.float32)[:, None],
        axis=0,
    )
    b_float = input_state_map.astype(jnp.float32)
    c_float = output_state_map.astype(jnp.float32)
    act_heads = activations.reshape(tokens, heads_dev, HEAD)
    scaled = act_heads.astype(jnp.float32) * input_scale[None, :, None]
    span_rows = min(512, tokens)
    span_count = tokens // span_rows
    causal = jnp.arange(span_rows)[:, None] >= jnp.arange(span_rows)[None, :]
    zero_level = jnp.zeros((heads_dev,), jnp.float32)
    carry_state = jnp.zeros((heads_dev, HEAD, STATE), jnp.float32)
    pieces = []
    for position in range(span_count):
        first_row = position * span_rows
        last_row = first_row + span_rows
        cum_block = cum_level[first_row:last_row]
        start_level = cum_level[first_row - 1] if position > 0 else zero_level
        scores = jnp.dot(
            output_state_map[first_row:last_row],
            input_state_map[first_row:last_row].T,
            preferred_element_type=jnp.float32,
        )
        weights = mixing(cum_block, scores, causal)
        weight_high, weight_low = split_parts(weights)
        x_span = act_heads[first_row:last_row]
        inner_part = jnp.einsum(
            "hts,shp->thp", weight_high, x_span, preferred_element_type=jnp.float32
        )
        inner_part = inner_part + jnp.einsum(
            "hts,shp->thp", weight_low, x_span, preferred_element_type=jnp.float32
        )
        inner_part = inner_part * input_scale[None, :, None]
        carried = jnp.exp(cum_block - start_level[None, :])[:, :, None] * jnp.einsum(
            "tn,hpn->thp", c_float[first_row:last_row], carry_state, precision=highest
        )
        pieces.append(inner_part + carried)
        end_level = cum_block[-1]
        tail_decay = jnp.exp(end_level[None, :] - cum_block)
        carry_state = jnp.exp(end_level - start_level)[:, None, None] * carry_state + jnp.einsum(
            "shp,sn->hpn",
            scaled[first_row:last_row] * tail_decay[:, :, None],
            b_float[first_row:last_row],
            precision=highest,
        )
    flat_state = carry_state.reshape(heads_dev, HEAD * STATE)
    level_lanes = jnp.broadcast_to(cum_level[-1][:, None], (heads_dev, 128))
    joined_all = lax.all_gather(jnp.concatenate([flat_state, level_lanes], axis=1), "seq")
    state_all = joined_all[:, :, : HEAD * STATE]
    level_all = joined_all[:, :, HEAD * STATE]
    incoming = carried_sum(state_all, level_all, seq_index, True)
    incoming = incoming.reshape(heads_dev, HEAD, STATE)
    outputs = jnp.concatenate(pieces, axis=0) + jnp.exp(cum_level)[:, :, None] * jnp.einsum(
        "tn,hpn->thp", c_float, incoming, precision=highest
    )
    mixed_out = (activations.astype(jnp.float32) + outputs.reshape(tokens, slice_width)).astype(
        jnp.bfloat16
    )
    g_all, mixed_out = lax.optimization_barrier((g_all, mixed_out))
    h_pick = jnp.einsum(
        "eb,brf->erf",
        chosen,
        mixed_out.reshape(blocks_dev, BLOCK, slice_width),
        preferred_element_type=jnp.float32,
    ).astype(jnp.bfloat16)
    h_block = dispatch(h_pick, exp_index, exp_count, mp_count, my_slice)
    h_all = lax.all_gather(h_block, "seq", axis=0, tiled=True)
    present = jnp.any(route_table == exp_index, axis=1)
    slot_of = jnp.cumsum(present.astype(jnp.int32)) - 1
    select = ((slot_of[None, :] == jnp.arange(slot_total)[:, None]) & present[None, :]).astype(
        jnp.bfloat16
    )
    x_rows = compact(select, h_all, half_width)
    g_rows = compact(select, g_all, half_width)
    up_local = expert_up_weight[0]
    down_local = expert_down_weight[0]
    pre_act = mp_sum(jnp.dot(x_rows, up_local, preferred_element_type=jnp.float32))
    activation = jax.nn.silu(pre_act).astype(jnp.bfloat16)
    down_grad = jnp.einsum("tf,td->fd", activation, g_rows, preferred_element_type=jnp.float32)
    act_grad = mp_sum(
        jnp.einsum("td,fd->tf", g_rows, down_local, preferred_element_type=jnp.float32)
    )
    sigmoid_pre = jax.nn.sigmoid(pre_act)
    pre_grad = (act_grad * sigmoid_pre * (1.0 + pre_act * (1.0 - sigmoid_pre))).astype(jnp.bfloat16)
    up_grad = jnp.einsum("td,tf->df", x_rows, pre_grad, preferred_element_type=jnp.float32)
    row_grad = jnp.einsum("tf,df->td", pre_grad, up_local, preferred_element_type=jnp.float32)
    row_grad = row_grad.astype(jnp.bfloat16).reshape(slot_total, BLOCK, half_width)
    spread_rows = jnp.einsum("js,jrf->srf", select, row_grad, preferred_element_type=jnp.float32)
    back_rows = lax.psum_scatter(
        spread_rows.reshape(BLOCK * lax.axis_size("seq"), half_width).astype(jnp.bfloat16),
        "seq",
        scatter_dimension=0,
        tiled=True,
    )
    returned = give_back(back_rows, exp_index, exp_count, mp_count)
    position = my_slice % exp_count
    chosen_by_shift = jnp.take(chosen, (position + jnp.arange(exp_count)) % exp_count, axis=0)
    token_grad = jnp.einsum(
        "kb,krf->brf", chosen_by_shift, returned, preferred_element_type=jnp.float32
    )
    total_grad = output_gradient.astype(jnp.float32) + token_grad.reshape(tokens, slice_width)
    grad_view = total_grad.reshape(tokens, heads_dev, HEAD)
    adjoint = jnp.zeros((heads_dev, HEAD, STATE), jnp.float32)
    back_pieces = [None] * span_count
    for position in reversed(range(span_count)):
        first_row = position * span_rows
        last_row = first_row + span_rows
        cum_block = cum_level[first_row:last_row]
        start_level = cum_level[first_row - 1] if position > 0 else zero_level
        scores = jnp.dot(
            output_state_map[first_row:last_row],
            input_state_map[first_row:last_row].T,
            preferred_element_type=jnp.float32,
        )
        weights = mixing(cum_block, scores, causal)
        weight_high, weight_low = split_parts(weights)
        grad_high, grad_low = split_parts(grad_view[first_row:last_row])
        inner_part = jnp.einsum(
            "hts,thp->shp", weight_high, grad_high, preferred_element_type=jnp.float32
        )
        inner_part = inner_part + jnp.einsum(
            "hts,thp->shp", weight_high, grad_low, preferred_element_type=jnp.float32
        )
        inner_part = inner_part + jnp.einsum(
            "hts,thp->shp", weight_low, grad_high, preferred_element_type=jnp.float32
        )
        end_level = cum_block[-1]
        tail_decay = jnp.exp(end_level[None, :] - cum_block)
        carried = tail_decay[:, :, None] * jnp.einsum(
            "sn,hpn->shp", b_float[first_row:last_row], adjoint, precision=highest
        )
        back_pieces[position] = inner_part + carried
        lead_decay = jnp.exp(cum_block - start_level[None, :])
        adjoint = jnp.exp(end_level - start_level)[:, None, None] * adjoint + jnp.einsum(
            "rhp,rn->hpn",
            grad_view[first_row:last_row] * lead_decay[:, :, None],
            c_float[first_row:last_row],
            precision=highest,
        )
    flat_adjoint = adjoint.reshape(heads_dev, HEAD * STATE)
    adjoint_all = lax.all_gather(flat_adjoint.astype(jnp.bfloat16), "seq")
    later_adjoint = carried_sum(adjoint_all, level_all, seq_index, False)
    later_adjoint = later_adjoint.reshape(heads_dev, HEAD, STATE)
    scan_grad = jnp.concatenate(back_pieces, axis=0) + jnp.exp(cum_level[-1][None, :] - cum_level)[
        :, :, None
    ] * jnp.einsum("sn,hpn->shp", b_float, later_adjoint, precision=highest)
    grad_x = total_grad + (input_scale[None, :, None] * scan_grad).reshape(tokens, slice_width)
    return (grad_x, up_grad[None], down_grad[None])


def solution(mesh):
    in_specs = (
        P("seq", ("expert", "mp")),
        P("seq", ("expert", "mp")),
        P("seq", None),
        P("seq", None),
        P(("expert", "mp")),
        P("seq"),
        P(),
        P("expert", "mp", "seq"),
        P("expert", "seq", "mp"),
    )
    out_specs = (P("seq", ("expert", "mp")), P("expert", "mp", "seq"), P("expert", "seq", "mp"))
    return jax.shard_map(
        per_device, mesh=mesh, in_specs=in_specs, out_specs=out_specs, check_vma=False
    )
```

```python
import jax
import jax.numpy as jnp
from jax import lax
from jax.sharding import PartitionSpec as P

HEAD = 64
STATE = 16
BLOCK = 128


spike_position_step = 0.3
highest = lax.Precision.HIGHEST


def carried_sum(values_all, level_all, own, earlier):
    count = level_all.shape[0]
    ids = jnp.arange(count)
    j, k = ids[:, None], ids[None, :]
    if earlier:
        between = (j < k) & (k < own)
        valid = ids < own
    else:
        between = (own < k) & (k < j)
        valid = ids > own
    exponent = jnp.sum(jnp.where(between[:, :, None], level_all[None], 0.0), axis=1)
    weight = jnp.where(valid[:, None], jnp.exp(exponent), 0.0)
    return jnp.sum(weight[:, :, None] * values_all.astype(jnp.float32), axis=0)


def mp_sum(part):
    part = part.astype(jnp.bfloat16)
    count = lax.axis_size("mp")
    total = part.astype(jnp.float32)
    for shift in range(1, count):
        pairs = [(src, (src + shift) % count) for src in range(count)]
        total = total + lax.ppermute(part, "mp", pairs).astype(jnp.float32)
    return total


def dispatch_pairs(exp_count, mp_count, shift):
    return [
        (src, ((src % exp_count + shift) % exp_count) * mp_count + src // exp_count)
        for src in range(exp_count * mp_count)
    ]


def dispatch(picks, exp_index, exp_count, mp_count, my_slice):
    position = my_slice % exp_count
    received = []
    for shift in range(exp_count):
        send = lax.dynamic_index_in_dim(picks, (position + shift) % exp_count, 0, keepdims=False)
        pairs = dispatch_pairs(exp_count, mp_count, shift)
        received.append(lax.ppermute(send, ("expert", "mp"), pairs))
    received = jnp.stack(received)
    order = (exp_index - jnp.arange(exp_count)) % exp_count
    placed = jnp.take(received, order, axis=0)
    rows, width = placed.shape[1], placed.shape[2]
    return placed.transpose(1, 0, 2).reshape(rows, exp_count * width)


def give_back(rows_half, exp_index, exp_count, mp_count):
    width = rows_half.shape[1] // exp_count
    pieces = rows_half.reshape(rows_half.shape[0], exp_count, width)
    received = []
    for shift in range(exp_count):
        column = (exp_index - shift) % exp_count
        send = lax.dynamic_index_in_dim(pieces, column, 1, keepdims=False)
        pairs = [(dst, src) for src, dst in dispatch_pairs(exp_count, mp_count, shift)]
        received.append(lax.ppermute(send, ("expert", "mp"), pairs))
    return jnp.stack(received)


def rounded(rounded_in):
    return lax.optimization_barrier(rounded_in.astype(jnp.bfloat16)).astype(jnp.float32)


def split_parts(values):
    high_part = values.astype(jnp.bfloat16)
    low_part = (values - high_part.astype(jnp.float32)).astype(jnp.bfloat16)
    return (high_part, low_part)


def mixing(cum_block, scores, causal):
    spread = cum_block.T[:, :, None] - cum_block.T[:, None, :]
    spread = jnp.where(causal[None], spread, -jnp.inf)
    return jnp.exp(spread) * scores[None]


def compact(select, gathered, half_width):
    blocks = gathered.reshape(select.shape[1], -1, half_width)
    used = jnp.any(select > 0, axis=1)
    source = jnp.argmax(select, axis=1)
    rows_out = [
        jnp.where(used[slot], lax.dynamic_index_in_dim(blocks, source[slot], 0, keepdims=False), 0)
        for slot in range(select.shape[0])
    ]
    return jnp.concatenate(rows_out, axis=0).astype(jnp.bfloat16)


def spread(present, slot_of, rows, half_width):
    blocks = rows.reshape(-1, BLOCK, half_width)
    placed = [
        jnp.where(
            present[shard],
            lax.dynamic_index_in_dim(blocks, jnp.maximum(slot_of[shard], 0), 0, keepdims=False),
            0,
        )
        for shard in range(present.shape[0])
    ]
    return jnp.concatenate(placed, axis=0).astype(jnp.bfloat16)


def per_device(
    activations,
    output_gradient,
    input_state_map,
    output_state_map,
    head_decay_speed,
    spike_decay_level,
    assign,
    expert_up_weight,
    expert_down_weight,
):
    tokens, slice_width = activations.shape
    heads_dev = slice_width // HEAD
    seq_count = lax.axis_size("seq")
    exp_count = lax.axis_size("expert")
    mp_count = lax.axis_size("mp")
    seq_index = lax.axis_index("seq")
    exp_index = lax.axis_index("expert")
    mp_index = lax.axis_index("mp")
    my_slice = exp_index * mp_count + mp_index
    half_width = slice_width * exp_count
    slot_total = seq_count // 2
    blocks_dev = tokens // BLOCK
    route_table = assign.reshape(seq_count, blocks_dev)
    own_row = lax.dynamic_index_in_dim(route_table, seq_index, 0, keepdims=False)
    chosen = (own_row[None, :] == jnp.arange(exp_count)[:, None]).astype(jnp.bfloat16)
    g_pick = jnp.einsum(
        "eb,brf->erf",
        chosen,
        output_gradient.reshape(blocks_dev, BLOCK, slice_width),
        preferred_element_type=jnp.float32,
    ).astype(jnp.bfloat16)
    g_block = dispatch(g_pick, exp_index, exp_count, mp_count, my_slice)
    g_all = lax.all_gather(g_block, "seq", axis=0)
    input_scale = jnp.sqrt(1.0 - jnp.exp(-2.0 * head_decay_speed))
    cum_level = jnp.cumsum(
        -head_decay_speed[None, :]
        - spike_position_step * spike_decay_level.astype(jnp.float32)[:, None],
        axis=0,
    )
    b_float = input_state_map.astype(jnp.float32)
    c_float = output_state_map.astype(jnp.float32)
    act_heads = activations.reshape(tokens, heads_dev, HEAD)
    scaled = act_heads.astype(jnp.float32) * input_scale[None, :, None]
    span_rows = min(512, tokens)
    span_count = tokens // span_rows
    causal = jnp.arange(span_rows)[:, None] >= jnp.arange(span_rows)[None, :]
    zero_level = jnp.zeros((heads_dev,), jnp.float32)
    carry_state = jnp.zeros((heads_dev, HEAD, STATE), jnp.float32)
    pieces = []
    for position in range(span_count):
        first_row = position * span_rows
        last_row = first_row + span_rows
        cum_block = cum_level[first_row:last_row]
        start_level = cum_level[first_row - 1] if position > 0 else zero_level
        scores = jnp.dot(
            output_state_map[first_row:last_row],
            input_state_map[first_row:last_row].T,
            preferred_element_type=jnp.float32,
        )
        weights = mixing(cum_block, scores, causal)
        weight_high, weight_low = split_parts(weights)
        x_span = act_heads[first_row:last_row]
        inner_part = jnp.einsum(
            "hts,shp->thp", weight_high, x_span, preferred_element_type=jnp.float32
        )
        inner_part = inner_part + jnp.einsum(
            "hts,shp->thp", weight_low, x_span, preferred_element_type=jnp.float32
        )
        inner_part = inner_part * input_scale[None, :, None]
        carried = jnp.exp(cum_block - start_level[None, :])[:, :, None] * jnp.einsum(
            "tn,hpn->thp", c_float[first_row:last_row], carry_state, precision=highest
        )
        pieces.append(inner_part + carried)
        end_level = cum_block[-1]
        tail_decay = jnp.exp(end_level[None, :] - cum_block)
        carry_state = jnp.exp(end_level - start_level)[:, None, None] * carry_state + jnp.einsum(
            "shp,sn->hpn",
            scaled[first_row:last_row] * tail_decay[:, :, None],
            b_float[first_row:last_row],
            precision=highest,
        )
    flat_state = carry_state.reshape(heads_dev, HEAD * STATE)
    level_lanes = jnp.broadcast_to(cum_level[-1][:, None], (heads_dev, 128))
    joined_all = lax.all_gather(jnp.concatenate([flat_state, level_lanes], axis=1), "seq")
    state_all = joined_all[:, :, : HEAD * STATE]
    level_all = joined_all[:, :, HEAD * STATE]
    incoming = carried_sum(state_all, level_all, seq_index, True)
    incoming = incoming.reshape(heads_dev, HEAD, STATE)
    outputs = jnp.concatenate(pieces, axis=0) + jnp.exp(cum_level)[:, :, None] * jnp.einsum(
        "tn,hpn->thp", c_float, incoming, precision=highest
    )
    mixed_out = (activations.astype(jnp.float32) + outputs.reshape(tokens, slice_width)).astype(
        jnp.bfloat16
    )
    g_all, mixed_out = lax.optimization_barrier((g_all, mixed_out))
    h_pick = jnp.einsum(
        "eb,brf->erf",
        chosen,
        mixed_out.reshape(blocks_dev, BLOCK, slice_width),
        preferred_element_type=jnp.float32,
    ).astype(jnp.bfloat16)
    h_block = dispatch(h_pick, exp_index, exp_count, mp_count, my_slice)
    h_all = lax.all_gather(h_block, "seq", axis=0)
    present = jnp.any(route_table == exp_index, axis=1)
    slot_of = jnp.cumsum(present.astype(jnp.int32)) - 1
    select = ((slot_of[None, :] == jnp.arange(slot_total)[:, None]) & present[None, :]).astype(
        jnp.bfloat16
    )
    x_rows = compact(select, h_all, half_width)
    g_rows = compact(select, g_all, half_width)
    up_local = expert_up_weight[0]
    down_local = expert_down_weight[0]
    pre_act = mp_sum(jnp.dot(x_rows, up_local, preferred_element_type=jnp.float32))
    activation = jax.nn.silu(pre_act).astype(jnp.bfloat16)
    down_grad = jnp.einsum("tf,td->fd", activation, g_rows, preferred_element_type=jnp.float32)
    act_grad = mp_sum(
        jnp.einsum("td,fd->tf", g_rows, down_local, preferred_element_type=jnp.float32)
    )
    sigmoid_pre = jax.nn.sigmoid(pre_act)
    pre_grad = (act_grad * sigmoid_pre * (1.0 + pre_act * (1.0 - sigmoid_pre))).astype(jnp.bfloat16)
    up_grad = jnp.einsum("td,tf->df", x_rows, pre_grad, preferred_element_type=jnp.float32)
    row_grad = jnp.einsum("tf,df->td", pre_grad, up_local, preferred_element_type=jnp.float32)
    spread_rows = spread(present, slot_of, row_grad.astype(jnp.bfloat16), half_width)
    back_rows = lax.psum_scatter(
        spread_rows,
        "seq",
        scatter_dimension=0,
        tiled=True,
    )
    returned = give_back(back_rows, exp_index, exp_count, mp_count)
    position = my_slice % exp_count
    chosen_by_shift = jnp.take(chosen, (position + jnp.arange(exp_count)) % exp_count, axis=0)
    token_grad = jnp.einsum(
        "kb,krf->brf", chosen_by_shift, returned, preferred_element_type=jnp.float32
    )
    total_grad = output_gradient.astype(jnp.float32) + token_grad.reshape(tokens, slice_width)
    grad_view = total_grad.reshape(tokens, heads_dev, HEAD)
    adjoint = jnp.zeros((heads_dev, HEAD, STATE), jnp.float32)
    back_pieces = [None] * span_count
    for position in reversed(range(span_count)):
        first_row = position * span_rows
        last_row = first_row + span_rows
        cum_block = cum_level[first_row:last_row]
        start_level = cum_level[first_row - 1] if position > 0 else zero_level
        scores = jnp.dot(
            output_state_map[first_row:last_row],
            input_state_map[first_row:last_row].T,
            preferred_element_type=jnp.float32,
        )
        weights = mixing(cum_block, scores, causal)
        weight_high, weight_low = split_parts(weights)
        grad_high, grad_low = split_parts(grad_view[first_row:last_row])
        inner_part = jnp.einsum(
            "hts,thp->shp", weight_high, grad_high, preferred_element_type=jnp.float32
        )
        inner_part = inner_part + jnp.einsum(
            "hts,thp->shp", weight_high, grad_low, preferred_element_type=jnp.float32
        )
        inner_part = inner_part + jnp.einsum(
            "hts,thp->shp", weight_low, grad_high, preferred_element_type=jnp.float32
        )
        end_level = cum_block[-1]
        tail_decay = jnp.exp(end_level[None, :] - cum_block)
        carried = tail_decay[:, :, None] * jnp.einsum(
            "sn,hpn->shp", b_float[first_row:last_row], adjoint, precision=highest
        )
        back_pieces[position] = inner_part + carried
        lead_decay = jnp.exp(cum_block - start_level[None, :])
        adjoint = jnp.exp(end_level - start_level)[:, None, None] * adjoint + jnp.einsum(
            "rhp,rn->hpn",
            grad_view[first_row:last_row] * lead_decay[:, :, None],
            c_float[first_row:last_row],
            precision=highest,
        )
    flat_adjoint = adjoint.reshape(heads_dev, HEAD * STATE)
    adjoint_all = lax.all_gather(flat_adjoint.astype(jnp.bfloat16), "seq")
    later_adjoint = carried_sum(adjoint_all, level_all, seq_index, False)
    later_adjoint = later_adjoint.reshape(heads_dev, HEAD, STATE)
    scan_grad = jnp.concatenate(back_pieces, axis=0) + jnp.exp(cum_level[-1][None, :] - cum_level)[
        :, :, None
    ] * jnp.einsum("sn,hpn->shp", b_float, later_adjoint, precision=highest)
    grad_x = total_grad + (input_scale[None, :, None] * scan_grad).reshape(tokens, slice_width)
    return (grad_x, up_grad[None], down_grad[None])


def solution(mesh):
    in_specs = (
        P("seq", ("expert", "mp")),
        P("seq", ("expert", "mp")),
        P("seq", None),
        P("seq", None),
        P(("expert", "mp")),
        P("seq"),
        P(),
        P("expert", "mp", "seq"),
        P("expert", "seq", "mp"),
    )
    out_specs = (P("seq", ("expert", "mp")), P("expert", "mp", "seq"), P("expert", "seq", "mp"))
    return jax.shard_map(
        per_device, mesh=mesh, in_specs=in_specs, out_specs=out_specs, check_vma=False
    )
```

```python
import jax
import jax.numpy as jnp
from jax import lax
from jax.sharding import PartitionSpec as P

HEAD = 64
STATE = 16
BLOCK = 128


spike_position_step = 0.3
highest = lax.Precision.HIGHEST


def carried_sum(values_all, level_all, own, earlier):
    count = level_all.shape[0]
    ids = jnp.arange(count)
    j, k = ids[:, None], ids[None, :]
    if earlier:
        between = (j < k) & (k < own)
        valid = ids < own
    else:
        between = (own < k) & (k < j)
        valid = ids > own
    exponent = jnp.sum(jnp.where(between[:, :, None], level_all[None], 0.0), axis=1)
    weight = jnp.where(valid[:, None], jnp.exp(exponent), 0.0)
    return jnp.sum(weight[:, :, None] * values_all.astype(jnp.float32), axis=0)


def mp_sum(part):
    part = part.astype(jnp.bfloat16)
    count = lax.axis_size("mp")
    total = part.astype(jnp.float32)
    for shift in range(1, count):
        pairs = [(src, (src + shift) % count) for src in range(count)]
        total = total + lax.ppermute(part, "mp", pairs).astype(jnp.float32)
    return total


def dispatch_pairs(exp_count, mp_count, shift):
    return [
        (src, ((src % exp_count + shift) % exp_count) * mp_count + src // exp_count)
        for src in range(exp_count * mp_count)
    ]


def dispatch(picks, exp_index, exp_count, mp_count, my_slice):
    position = my_slice % exp_count
    received = []
    for shift in range(exp_count):
        send = lax.dynamic_index_in_dim(picks, (position + shift) % exp_count, 0, keepdims=False)
        pairs = dispatch_pairs(exp_count, mp_count, shift)
        received.append(lax.ppermute(send, ("expert", "mp"), pairs))
    received = jnp.stack(received)
    order = (exp_index - jnp.arange(exp_count)) % exp_count
    placed = jnp.take(received, order, axis=0)
    rows, width = placed.shape[1], placed.shape[2]
    return placed.transpose(1, 0, 2).reshape(rows, exp_count * width)


def give_back(rows_half, exp_index, exp_count, mp_count):
    width = rows_half.shape[1] // exp_count
    pieces = rows_half.reshape(rows_half.shape[0], exp_count, width)
    received = []
    for shift in range(exp_count):
        column = (exp_index - shift) % exp_count
        send = lax.dynamic_index_in_dim(pieces, column, 1, keepdims=False)
        pairs = [(dst, src) for src, dst in dispatch_pairs(exp_count, mp_count, shift)]
        received.append(lax.ppermute(send, ("expert", "mp"), pairs))
    return jnp.stack(received)


def rounded(rounded_in):
    return lax.optimization_barrier(rounded_in.astype(jnp.bfloat16)).astype(jnp.float32)


def split_parts(values):
    high_part = values.astype(jnp.bfloat16)
    low_part = (values - high_part.astype(jnp.float32)).astype(jnp.bfloat16)
    return (high_part, low_part)


def mixing(cum_block, scores, causal):
    spread = cum_block.T[:, :, None] - cum_block.T[:, None, :]
    spread = jnp.where(causal[None], spread, -jnp.inf)
    return jnp.exp(spread) * scores[None]


def compact(select, gathered, half_width):
    blocks = gathered.reshape(select.shape[1], -1, half_width)
    used = jnp.any(select > 0, axis=1)
    source = jnp.argmax(select, axis=1)
    rows_out = [
        jnp.where(used[slot], lax.dynamic_index_in_dim(blocks, source[slot], 0, keepdims=False), 0)
        for slot in range(select.shape[0])
    ]
    return jnp.concatenate(rows_out, axis=0).astype(jnp.bfloat16)


def spread(present, slot_of, rows, half_width, block_rows):
    blocks = rows.reshape(-1, block_rows, half_width)
    placed = [
        jnp.where(
            present[shard],
            lax.dynamic_index_in_dim(blocks, jnp.maximum(slot_of[shard], 0), 0, keepdims=False),
            0,
        )
        for shard in range(present.shape[0])
    ]
    return jnp.concatenate(placed, axis=0).astype(jnp.bfloat16)


def per_device(
    activations,
    output_gradient,
    input_state_map,
    output_state_map,
    head_decay_speed,
    spike_decay_level,
    assign,
    expert_up_weight,
    expert_down_weight,
):
    tokens, slice_width = activations.shape
    heads_dev = slice_width // HEAD
    seq_count = lax.axis_size("seq")
    exp_count = lax.axis_size("expert")
    mp_count = lax.axis_size("mp")
    seq_index = lax.axis_index("seq")
    exp_index = lax.axis_index("expert")
    mp_index = lax.axis_index("mp")
    my_slice = exp_index * mp_count + mp_index
    half_width = slice_width * exp_count
    slot_total = seq_count // 2
    blocks_dev = tokens // BLOCK
    route_table = assign.reshape(seq_count, blocks_dev)
    own_row = lax.dynamic_index_in_dim(route_table, seq_index, 0, keepdims=False)
    chosen = (own_row[None, :] == jnp.arange(exp_count)[:, None]).astype(jnp.bfloat16)
    g_pick = jnp.einsum(
        "eb,brf->erf",
        chosen,
        output_gradient.reshape(blocks_dev, BLOCK, slice_width),
        preferred_element_type=jnp.float32,
    ).astype(jnp.bfloat16)
    g_block = dispatch(g_pick, exp_index, exp_count, mp_count, my_slice)
    g_all = lax.all_gather(g_block, "seq", axis=0)
    input_scale = jnp.sqrt(1.0 - jnp.exp(-2.0 * head_decay_speed))
    cum_level = jnp.cumsum(
        -head_decay_speed[None, :]
        - spike_position_step * spike_decay_level.astype(jnp.float32)[:, None],
        axis=0,
    )
    b_float = input_state_map.astype(jnp.float32)
    c_float = output_state_map.astype(jnp.float32)
    act_heads = activations.reshape(tokens, heads_dev, HEAD)
    scaled = act_heads.astype(jnp.float32) * input_scale[None, :, None]
    span_rows = min(512, tokens)
    span_count = tokens // span_rows
    causal = jnp.arange(span_rows)[:, None] >= jnp.arange(span_rows)[None, :]
    zero_level = jnp.zeros((heads_dev,), jnp.float32)
    carry_state = jnp.zeros((heads_dev, HEAD, STATE), jnp.float32)
    pieces = []
    for position in range(span_count):
        first_row = position * span_rows
        last_row = first_row + span_rows
        cum_block = cum_level[first_row:last_row]
        start_level = cum_level[first_row - 1] if position > 0 else zero_level
        scores = jnp.dot(
            output_state_map[first_row:last_row],
            input_state_map[first_row:last_row].T,
            preferred_element_type=jnp.float32,
        )
        weights = mixing(cum_block, scores, causal)
        weight_high, weight_low = split_parts(weights)
        x_span = act_heads[first_row:last_row]
        inner_part = jnp.einsum(
            "hts,shp->thp", weight_high, x_span, preferred_element_type=jnp.float32
        )
        inner_part = inner_part + jnp.einsum(
            "hts,shp->thp", weight_low, x_span, preferred_element_type=jnp.float32
        )
        inner_part = inner_part * input_scale[None, :, None]
        carried = jnp.exp(cum_block - start_level[None, :])[:, :, None] * jnp.einsum(
            "tn,hpn->thp", c_float[first_row:last_row], carry_state, precision=highest
        )
        pieces.append(inner_part + carried)
        end_level = cum_block[-1]
        tail_decay = jnp.exp(end_level[None, :] - cum_block)
        carry_state = jnp.exp(end_level - start_level)[:, None, None] * carry_state + jnp.einsum(
            "shp,sn->hpn",
            scaled[first_row:last_row] * tail_decay[:, :, None],
            b_float[first_row:last_row],
            precision=highest,
        )
    flat_state = carry_state.reshape(heads_dev, HEAD * STATE)
    level_lanes = jnp.broadcast_to(cum_level[-1][:, None], (heads_dev, 128))
    joined_all = lax.all_gather(jnp.concatenate([flat_state, level_lanes], axis=1), "seq")
    state_all = joined_all[:, :, : HEAD * STATE]
    level_all = joined_all[:, :, HEAD * STATE]
    incoming = carried_sum(state_all, level_all, seq_index, True)
    incoming = incoming.reshape(heads_dev, HEAD, STATE)
    outputs = jnp.concatenate(pieces, axis=0) + jnp.exp(cum_level)[:, :, None] * jnp.einsum(
        "tn,hpn->thp", c_float, incoming, precision=highest
    )
    mixed_out = (activations.astype(jnp.float32) + outputs.reshape(tokens, slice_width)).astype(
        jnp.bfloat16
    )
    g_all, mixed_out = lax.optimization_barrier((g_all, mixed_out))
    h_pick = jnp.einsum(
        "eb,brf->erf",
        chosen,
        mixed_out.reshape(blocks_dev, BLOCK, slice_width),
        preferred_element_type=jnp.float32,
    ).astype(jnp.bfloat16)
    h_block = dispatch(h_pick, exp_index, exp_count, mp_count, my_slice)
    chunks = 2
    chunk_rows = BLOCK // chunks
    h_parts = [
        lax.all_gather(h_block[c * chunk_rows : (c + 1) * chunk_rows], "seq", axis=0)
        for c in range(chunks)
    ]
    present = jnp.any(route_table == exp_index, axis=1)
    slot_of = jnp.cumsum(present.astype(jnp.int32)) - 1
    select = ((slot_of[None, :] == jnp.arange(slot_total)[:, None]) & present[None, :]).astype(
        jnp.bfloat16
    )
    up_local = expert_up_weight[0]
    down_local = expert_down_weight[0]
    back_parts = []
    for c in range(chunks):
        x_rows = compact(select, h_parts[c], half_width)
        g_rows = compact(select, g_all[:, c * chunk_rows : (c + 1) * chunk_rows], half_width)
        pre_act = mp_sum(jnp.dot(x_rows, up_local, preferred_element_type=jnp.float32))
        activation = jax.nn.silu(pre_act).astype(jnp.bfloat16)
        down_part = jnp.einsum("tf,td->fd", activation, g_rows, preferred_element_type=jnp.float32)
        act_grad = mp_sum(
            jnp.einsum("td,fd->tf", g_rows, down_local, preferred_element_type=jnp.float32)
        )
        sigmoid_pre = jax.nn.sigmoid(pre_act)
        pre_grad = (act_grad * sigmoid_pre * (1.0 + pre_act * (1.0 - sigmoid_pre))).astype(
            jnp.bfloat16
        )
        up_part = jnp.einsum("td,tf->df", x_rows, pre_grad, preferred_element_type=jnp.float32)
        down_grad = down_part if c == 0 else down_grad + down_part
        up_grad = up_part if c == 0 else up_grad + up_part
        row_grad = jnp.einsum("tf,df->td", pre_grad, up_local, preferred_element_type=jnp.float32)
        spread_rows = spread(present, slot_of, row_grad.astype(jnp.bfloat16), half_width, chunk_rows)
        back_parts.append(lax.psum_scatter(spread_rows, "seq", scatter_dimension=0, tiled=True))
    back_rows = jnp.concatenate(back_parts, axis=0)
    returned = give_back(back_rows, exp_index, exp_count, mp_count)
    position = my_slice % exp_count
    chosen_by_shift = jnp.take(chosen, (position + jnp.arange(exp_count)) % exp_count, axis=0)
    token_grad = jnp.einsum(
        "kb,krf->brf", chosen_by_shift, returned, preferred_element_type=jnp.float32
    )
    total_grad = output_gradient.astype(jnp.float32) + token_grad.reshape(tokens, slice_width)
    grad_view = total_grad.reshape(tokens, heads_dev, HEAD)
    adjoint = jnp.zeros((heads_dev, HEAD, STATE), jnp.float32)
    back_pieces = [None] * span_count
    for position in reversed(range(span_count)):
        first_row = position * span_rows
        last_row = first_row + span_rows
        cum_block = cum_level[first_row:last_row]
        start_level = cum_level[first_row - 1] if position > 0 else zero_level
        scores = jnp.dot(
            output_state_map[first_row:last_row],
            input_state_map[first_row:last_row].T,
            preferred_element_type=jnp.float32,
        )
        weights = mixing(cum_block, scores, causal)
        weight_high, weight_low = split_parts(weights)
        grad_high, grad_low = split_parts(grad_view[first_row:last_row])
        inner_part = jnp.einsum(
            "hts,thp->shp", weight_high, grad_high, preferred_element_type=jnp.float32
        )
        inner_part = inner_part + jnp.einsum(
            "hts,thp->shp", weight_high, grad_low, preferred_element_type=jnp.float32
        )
        inner_part = inner_part + jnp.einsum(
            "hts,thp->shp", weight_low, grad_high, preferred_element_type=jnp.float32
        )
        end_level = cum_block[-1]
        tail_decay = jnp.exp(end_level[None, :] - cum_block)
        carried = tail_decay[:, :, None] * jnp.einsum(
            "sn,hpn->shp", b_float[first_row:last_row], adjoint, precision=highest
        )
        back_pieces[position] = inner_part + carried
        lead_decay = jnp.exp(cum_block - start_level[None, :])
        adjoint = jnp.exp(end_level - start_level)[:, None, None] * adjoint + jnp.einsum(
            "rhp,rn->hpn",
            grad_view[first_row:last_row] * lead_decay[:, :, None],
            c_float[first_row:last_row],
            precision=highest,
        )
    flat_adjoint = adjoint.reshape(heads_dev, HEAD * STATE)
    adjoint_all = lax.all_gather(flat_adjoint.astype(jnp.bfloat16), "seq")
    later_adjoint = carried_sum(adjoint_all, level_all, seq_index, False)
    later_adjoint = later_adjoint.reshape(heads_dev, HEAD, STATE)
    scan_grad = jnp.concatenate(back_pieces, axis=0) + jnp.exp(cum_level[-1][None, :] - cum_level)[
        :, :, None
    ] * jnp.einsum("sn,hpn->shp", b_float, later_adjoint, precision=highest)
    grad_x = total_grad + (input_scale[None, :, None] * scan_grad).reshape(tokens, slice_width)
    return (grad_x, up_grad[None], down_grad[None])


def solution(mesh):
    in_specs = (
        P("seq", ("expert", "mp")),
        P("seq", ("expert", "mp")),
        P("seq", None),
        P("seq", None),
        P(("expert", "mp")),
        P("seq"),
        P(),
        P("expert", "mp", "seq"),
        P("expert", "seq", "mp"),
    )
    out_specs = (P("seq", ("expert", "mp")), P("expert", "mp", "seq"), P("expert", "seq", "mp"))
    return jax.shard_map(
        per_device, mesh=mesh, in_specs=in_specs, out_specs=out_specs, check_vma=False
    )
```

```python
import jax
import jax.numpy as jnp
from jax import lax
from jax.sharding import PartitionSpec as P

HEAD = 64
STATE = 16
BLOCK = 128


spike_position_step = 0.3
highest = lax.Precision.HIGHEST


def carried_sum(values_all, level_all, own, earlier):
    count = level_all.shape[0]
    ids = jnp.arange(count)
    j, k = ids[:, None], ids[None, :]
    if earlier:
        between = (j < k) & (k < own)
        valid = ids < own
    else:
        between = (own < k) & (k < j)
        valid = ids > own
    exponent = jnp.sum(jnp.where(between[:, :, None], level_all[None], 0.0), axis=1)
    weight = jnp.where(valid[:, None], jnp.exp(exponent), 0.0)
    return jnp.sum(weight[:, :, None] * values_all.astype(jnp.float32), axis=0)


def mp_sum(part):
    part = part.astype(jnp.bfloat16)
    count = lax.axis_size("mp")
    total = part.astype(jnp.float32)
    for shift in range(1, count):
        pairs = [(src, (src + shift) % count) for src in range(count)]
        total = total + lax.ppermute(part, "mp", pairs).astype(jnp.float32)
    return total


def dispatch_pairs(exp_count, mp_count, shift):
    return [
        (src, ((src % exp_count + shift) % exp_count) * mp_count + src // exp_count)
        for src in range(exp_count * mp_count)
    ]


def dispatch(picks, exp_index, exp_count, mp_count, my_slice):
    position = my_slice % exp_count
    received = []
    for shift in range(exp_count):
        send = lax.dynamic_index_in_dim(picks, (position + shift) % exp_count, 0, keepdims=False)
        pairs = dispatch_pairs(exp_count, mp_count, shift)
        received.append(lax.ppermute(send, ("expert", "mp"), pairs))
    received = jnp.stack(received)
    order = (exp_index - jnp.arange(exp_count)) % exp_count
    placed = jnp.take(received, order, axis=0)
    rows, width = placed.shape[1], placed.shape[2]
    return placed.transpose(1, 0, 2).reshape(rows, exp_count * width)


def give_back(rows_half, exp_index, exp_count, mp_count):
    width = rows_half.shape[1] // exp_count
    pieces = rows_half.reshape(rows_half.shape[0], exp_count, width)
    received = []
    for shift in range(exp_count):
        column = (exp_index - shift) % exp_count
        send = lax.dynamic_index_in_dim(pieces, column, 1, keepdims=False)
        pairs = [(dst, src) for src, dst in dispatch_pairs(exp_count, mp_count, shift)]
        received.append(lax.ppermute(send, ("expert", "mp"), pairs))
    return jnp.stack(received)


def rounded(rounded_in):
    return lax.optimization_barrier(rounded_in.astype(jnp.bfloat16)).astype(jnp.float32)


def split_parts(values):
    high_part = values.astype(jnp.bfloat16)
    low_part = (values - high_part.astype(jnp.float32)).astype(jnp.bfloat16)
    return (high_part, low_part)


def mixing(cum_block, scores, causal):
    spread = cum_block.T[:, :, None] - cum_block.T[:, None, :]
    spread = jnp.where(causal[None], spread, -jnp.inf)
    return jnp.exp(spread) * scores[None]


def compact(select, gathered, half_width):
    blocks = gathered.reshape(select.shape[1], -1, half_width)
    used = jnp.any(select > 0, axis=1)
    source = jnp.argmax(select, axis=1)
    rows_out = jnp.where(used[:, None, None], jnp.take(blocks, source, axis=0, mode="clip"), 0)
    return rows_out.reshape(-1, half_width).astype(jnp.bfloat16)


def spread(present, slot_of, rows, half_width):
    blocks = rows.reshape(-1, BLOCK, half_width)
    placed = jnp.take(blocks, jnp.maximum(slot_of, 0), axis=0, mode="clip")
    placed = jnp.where(present[:, None, None], placed, 0)
    return placed.reshape(-1, half_width).astype(jnp.bfloat16)


def per_device(
    activations,
    output_gradient,
    input_state_map,
    output_state_map,
    head_decay_speed,
    spike_decay_level,
    assign,
    expert_up_weight,
    expert_down_weight,
):
    tokens, slice_width = activations.shape
    heads_dev = slice_width // HEAD
    seq_count = lax.axis_size("seq")
    exp_count = lax.axis_size("expert")
    mp_count = lax.axis_size("mp")
    seq_index = lax.axis_index("seq")
    exp_index = lax.axis_index("expert")
    mp_index = lax.axis_index("mp")
    my_slice = exp_index * mp_count + mp_index
    half_width = slice_width * exp_count
    slot_total = seq_count // 2
    blocks_dev = tokens // BLOCK
    route_table = assign.reshape(seq_count, blocks_dev)
    own_row = lax.dynamic_index_in_dim(route_table, seq_index, 0, keepdims=False)
    chosen = (own_row[None, :] == jnp.arange(exp_count)[:, None]).astype(jnp.bfloat16)
    g_pick = jnp.einsum(
        "eb,brf->erf",
        chosen,
        output_gradient.reshape(blocks_dev, BLOCK, slice_width),
        preferred_element_type=jnp.float32,
    ).astype(jnp.bfloat16)
    g_block = dispatch(g_pick, exp_index, exp_count, mp_count, my_slice)
    g_all = lax.all_gather(g_block, "seq", axis=0)
    present = jnp.any(route_table == exp_index, axis=1)
    slot_of = jnp.cumsum(present.astype(jnp.int32)) - 1
    select = ((slot_of[None, :] == jnp.arange(slot_total)[:, None]) & present[None, :]).astype(
        jnp.bfloat16
    )
    g_rows = compact(select, g_all, half_width)
    input_scale = jnp.sqrt(1.0 - jnp.exp(-2.0 * head_decay_speed))
    cum_level = jnp.cumsum(
        -head_decay_speed[None, :]
        - spike_position_step * spike_decay_level.astype(jnp.float32)[:, None],
        axis=0,
    )
    b_float = input_state_map.astype(jnp.float32)
    c_float = output_state_map.astype(jnp.float32)
    act_heads = activations.reshape(tokens, heads_dev, HEAD)
    scaled = act_heads.astype(jnp.float32) * input_scale[None, :, None]
    span_rows = min(512, tokens)
    span_count = tokens // span_rows
    causal = jnp.arange(span_rows)[:, None] >= jnp.arange(span_rows)[None, :]
    zero_level = jnp.zeros((heads_dev,), jnp.float32)
    carry_state = jnp.zeros((heads_dev, HEAD, STATE), jnp.float32)
    pieces = []
    for position in range(span_count):
        first_row = position * span_rows
        last_row = first_row + span_rows
        cum_block = cum_level[first_row:last_row]
        start_level = cum_level[first_row - 1] if position > 0 else zero_level
        scores = jnp.dot(
            output_state_map[first_row:last_row],
            input_state_map[first_row:last_row].T,
            preferred_element_type=jnp.float32,
        )
        weights = mixing(cum_block, scores, causal)
        weight_high, weight_low = split_parts(weights)
        x_span = act_heads[first_row:last_row]
        inner_part = jnp.einsum(
            "hts,shp->thp", weight_high, x_span, preferred_element_type=jnp.float32
        )
        inner_part = inner_part + jnp.einsum(
            "hts,shp->thp", weight_low, x_span, preferred_element_type=jnp.float32
        )
        inner_part = inner_part * input_scale[None, :, None]
        carried = jnp.exp(cum_block - start_level[None, :])[:, :, None] * jnp.einsum(
            "tn,hpn->thp", c_float[first_row:last_row], carry_state, precision=highest
        )
        pieces.append(inner_part + carried)
        end_level = cum_block[-1]
        tail_decay = jnp.exp(end_level[None, :] - cum_block)
        carry_state = jnp.exp(end_level - start_level)[:, None, None] * carry_state + jnp.einsum(
            "shp,sn->hpn",
            scaled[first_row:last_row] * tail_decay[:, :, None],
            b_float[first_row:last_row],
            precision=highest,
        )
    flat_state = carry_state.reshape(heads_dev, HEAD * STATE)
    level_lanes = jnp.broadcast_to(cum_level[-1][:, None], (heads_dev, 128))
    joined_all = lax.all_gather(jnp.concatenate([flat_state, level_lanes], axis=1), "seq")
    state_all = joined_all[:, :, : HEAD * STATE]
    level_all = joined_all[:, :, HEAD * STATE]
    incoming = carried_sum(state_all, level_all, seq_index, True)
    incoming = incoming.reshape(heads_dev, HEAD, STATE)
    outputs = jnp.concatenate(pieces, axis=0) + jnp.exp(cum_level)[:, :, None] * jnp.einsum(
        "tn,hpn->thp", c_float, incoming, precision=highest
    )
    mixed_out = (activations.astype(jnp.float32) + outputs.reshape(tokens, slice_width)).astype(
        jnp.bfloat16
    )
    g_rows, mixed_out = lax.optimization_barrier((g_rows, mixed_out))
    h_pick = jnp.einsum(
        "eb,brf->erf",
        chosen,
        mixed_out.reshape(blocks_dev, BLOCK, slice_width),
        preferred_element_type=jnp.float32,
    ).astype(jnp.bfloat16)
    h_block = dispatch(h_pick, exp_index, exp_count, mp_count, my_slice)
    h_all = lax.all_gather(h_block, "seq", axis=0)
    x_rows = compact(select, h_all, half_width)
    up_local = expert_up_weight[0]
    down_local = expert_down_weight[0]
    pre_act = mp_sum(jnp.dot(x_rows, up_local, preferred_element_type=jnp.float32))
    activation = jax.nn.silu(pre_act).astype(jnp.bfloat16)
    down_grad = jnp.einsum("tf,td->fd", activation, g_rows, preferred_element_type=jnp.float32)
    act_grad = mp_sum(
        jnp.einsum("td,fd->tf", g_rows, down_local, preferred_element_type=jnp.float32)
    )
    sigmoid_pre = jax.nn.sigmoid(pre_act)
    pre_grad = (act_grad * sigmoid_pre * (1.0 + pre_act * (1.0 - sigmoid_pre))).astype(jnp.bfloat16)
    up_grad = jnp.einsum("td,tf->df", x_rows, pre_grad, preferred_element_type=jnp.float32)
    row_grad = jnp.einsum("tf,df->td", pre_grad, up_local, preferred_element_type=jnp.float32)
    spread_rows = spread(present, slot_of, row_grad.astype(jnp.bfloat16), half_width)
    back_rows = lax.psum_scatter(
        spread_rows,
        "seq",
        scatter_dimension=0,
        tiled=True,
    )
    returned = give_back(back_rows, exp_index, exp_count, mp_count)
    position = my_slice % exp_count
    chosen_by_shift = jnp.take(chosen, (position + jnp.arange(exp_count)) % exp_count, axis=0)
    token_grad = jnp.einsum(
        "kb,krf->brf", chosen_by_shift, returned, preferred_element_type=jnp.float32
    )
    total_grad = output_gradient.astype(jnp.float32) + token_grad.reshape(tokens, slice_width)
    grad_view = total_grad.reshape(tokens, heads_dev, HEAD)
    adjoint = jnp.zeros((heads_dev, HEAD, STATE), jnp.float32)
    back_pieces = [None] * span_count
    for position in reversed(range(span_count)):
        first_row = position * span_rows
        last_row = first_row + span_rows
        cum_block = cum_level[first_row:last_row]
        start_level = cum_level[first_row - 1] if position > 0 else zero_level
        scores = jnp.dot(
            output_state_map[first_row:last_row],
            input_state_map[first_row:last_row].T,
            preferred_element_type=jnp.float32,
        )
        weights = mixing(cum_block, scores, causal)
        weight_high, weight_low = split_parts(weights)
        grad_high, grad_low = split_parts(grad_view[first_row:last_row])
        inner_part = jnp.einsum(
            "hts,thp->shp", weight_high, grad_high, preferred_element_type=jnp.float32
        )
        inner_part = inner_part + jnp.einsum(
            "hts,thp->shp", weight_high, grad_low, preferred_element_type=jnp.float32
        )
        inner_part = inner_part + jnp.einsum(
            "hts,thp->shp", weight_low, grad_high, preferred_element_type=jnp.float32
        )
        end_level = cum_block[-1]
        tail_decay = jnp.exp(end_level[None, :] - cum_block)
        carried = tail_decay[:, :, None] * jnp.einsum(
            "sn,hpn->shp", b_float[first_row:last_row], adjoint, precision=highest
        )
        back_pieces[position] = inner_part + carried
        lead_decay = jnp.exp(cum_block - start_level[None, :])
        adjoint = jnp.exp(end_level - start_level)[:, None, None] * adjoint + jnp.einsum(
            "rhp,rn->hpn",
            grad_view[first_row:last_row] * lead_decay[:, :, None],
            c_float[first_row:last_row],
            precision=highest,
        )
    flat_adjoint = adjoint.reshape(heads_dev, HEAD * STATE)
    adjoint_all = lax.all_gather(flat_adjoint.astype(jnp.bfloat16), "seq")
    later_adjoint = carried_sum(adjoint_all, level_all, seq_index, False)
    later_adjoint = later_adjoint.reshape(heads_dev, HEAD, STATE)
    scan_grad = jnp.concatenate(back_pieces, axis=0) + jnp.exp(cum_level[-1][None, :] - cum_level)[
        :, :, None
    ] * jnp.einsum("sn,hpn->shp", b_float, later_adjoint, precision=highest)
    grad_x = total_grad + (input_scale[None, :, None] * scan_grad).reshape(tokens, slice_width)
    return (grad_x, up_grad[None], down_grad[None])


def solution(mesh):
    in_specs = (
        P("seq", ("expert", "mp")),
        P("seq", ("expert", "mp")),
        P("seq", None),
        P("seq", None),
        P(("expert", "mp")),
        P("seq"),
        P(),
        P("expert", "mp", "seq"),
        P("expert", "seq", "mp"),
    )
    out_specs = (P("seq", ("expert", "mp")), P("expert", "mp", "seq"), P("expert", "seq", "mp"))
    return jax.shard_map(
        per_device, mesh=mesh, in_specs=in_specs, out_specs=out_specs, check_vma=False
    )
```

```python
import jax
import jax.numpy as jnp
from jax import lax
from jax.sharding import PartitionSpec as P

HEAD = 64
STATE = 16
BLOCK = 128


spike_position_step = 0.3
highest = lax.Precision.HIGHEST


def carried_sum(values_all, level_all, own, earlier):
    count = level_all.shape[0]
    ids = jnp.arange(count)
    j, k = ids[:, None], ids[None, :]
    if earlier:
        between = (j < k) & (k < own)
        valid = ids < own
    else:
        between = (own < k) & (k < j)
        valid = ids > own
    exponent = jnp.sum(jnp.where(between[:, :, None], level_all[None], 0.0), axis=1)
    weight = jnp.where(valid[:, None], jnp.exp(exponent), 0.0)
    return jnp.sum(weight[:, :, None] * values_all.astype(jnp.float32), axis=0)


def mp_sum(part):
    part = part.astype(jnp.bfloat16)
    count = lax.axis_size("mp")
    total = part.astype(jnp.float32)
    for shift in range(1, count):
        pairs = [(src, (src + shift) % count) for src in range(count)]
        total = total + lax.ppermute(part, "mp", pairs).astype(jnp.float32)
    return total


def dispatch_pairs(exp_count, mp_count, shift):
    return [
        (src, ((src % exp_count + shift) % exp_count) * mp_count + src // exp_count)
        for src in range(exp_count * mp_count)
    ]


def dispatch(picks, exp_index, exp_count, mp_count, my_slice):
    position = my_slice % exp_count
    received = []
    for shift in range(exp_count):
        send = lax.dynamic_index_in_dim(picks, (position + shift) % exp_count, 0, keepdims=False)
        pairs = dispatch_pairs(exp_count, mp_count, shift)
        received.append(lax.ppermute(send, ("expert", "mp"), pairs))
    received = jnp.stack(received)
    order = (exp_index - jnp.arange(exp_count)) % exp_count
    placed = jnp.take(received, order, axis=0)
    rows, width = placed.shape[1], placed.shape[2]
    return placed.transpose(1, 0, 2).reshape(rows, exp_count * width)


def give_back(rows_half, exp_index, exp_count, mp_count):
    width = rows_half.shape[1] // exp_count
    pieces = rows_half.reshape(rows_half.shape[0], exp_count, width)
    received = []
    for shift in range(exp_count):
        column = (exp_index - shift) % exp_count
        send = lax.dynamic_index_in_dim(pieces, column, 1, keepdims=False)
        pairs = [(dst, src) for src, dst in dispatch_pairs(exp_count, mp_count, shift)]
        received.append(lax.ppermute(send, ("expert", "mp"), pairs))
    return jnp.stack(received)


def rounded(rounded_in):
    return lax.optimization_barrier(rounded_in.astype(jnp.bfloat16)).astype(jnp.float32)


def split_parts(values):
    high_part = values.astype(jnp.bfloat16)
    low_part = (values - high_part.astype(jnp.float32)).astype(jnp.bfloat16)
    return (high_part, low_part)


def mixing(cum_block, scores, causal):
    spread = cum_block.T[:, :, None] - cum_block.T[:, None, :]
    spread = jnp.where(causal[None], spread, -jnp.inf)
    return jnp.exp(spread) * scores[None]


def compact(select, gathered, half_width):
    blocks = gathered.reshape(select.shape[1], -1, half_width)
    used = jnp.any(select > 0, axis=1)
    source = jnp.argmax(select, axis=1)
    rows_out = jnp.where(used[:, None, None], jnp.take(blocks, source, axis=0, mode="clip"), 0)
    return rows_out.reshape(-1, half_width).astype(jnp.bfloat16)


def spread(present, slot_of, rows, half_width):
    blocks = rows.reshape(-1, BLOCK, half_width)
    placed = jnp.take(blocks, jnp.maximum(slot_of, 0), axis=0, mode="clip")
    placed = jnp.where(present[:, None, None], placed, 0)
    return placed.reshape(-1, half_width).astype(jnp.bfloat16)


def per_device(
    activations,
    output_gradient,
    input_state_map,
    output_state_map,
    head_decay_speed,
    spike_decay_level,
    assign,
    expert_up_weight,
    expert_down_weight,
):
    tokens, slice_width = activations.shape
    heads_dev = slice_width // HEAD
    seq_count = lax.axis_size("seq")
    exp_count = lax.axis_size("expert")
    mp_count = lax.axis_size("mp")
    seq_index = lax.axis_index("seq")
    exp_index = lax.axis_index("expert")
    mp_index = lax.axis_index("mp")
    my_slice = exp_index * mp_count + mp_index
    half_width = slice_width * exp_count
    slot_total = seq_count // 2
    blocks_dev = tokens // BLOCK
    route_table = assign.reshape(seq_count, blocks_dev)
    own_row = lax.dynamic_index_in_dim(route_table, seq_index, 0, keepdims=False)
    chosen = (own_row[None, :] == jnp.arange(exp_count)[:, None]).astype(jnp.bfloat16)
    g_pick = jnp.einsum(
        "eb,brf->erf",
        chosen,
        output_gradient.reshape(blocks_dev, BLOCK, slice_width),
        preferred_element_type=jnp.float32,
    ).astype(jnp.bfloat16)
    g_block = dispatch(g_pick, exp_index, exp_count, mp_count, my_slice)
    g_all = lax.all_gather(g_block, "seq", axis=0)
    present = jnp.any(route_table == exp_index, axis=1)
    slot_of = jnp.cumsum(present.astype(jnp.int32)) - 1
    select = ((slot_of[None, :] == jnp.arange(slot_total)[:, None]) & present[None, :]).astype(
        jnp.bfloat16
    )
    g_rows = compact(select, g_all, half_width)
    input_scale = jnp.sqrt(1.0 - jnp.exp(-2.0 * head_decay_speed))
    cum_level = jnp.cumsum(
        -head_decay_speed[None, :]
        - spike_position_step * spike_decay_level.astype(jnp.float32)[:, None],
        axis=0,
    )
    b_float = input_state_map.astype(jnp.float32)
    c_float = output_state_map.astype(jnp.float32)
    act_heads = activations.reshape(tokens, heads_dev, HEAD)
    scaled = act_heads.astype(jnp.float32) * input_scale[None, :, None]
    span_rows = min(512, tokens)
    span_count = tokens // span_rows
    causal = jnp.arange(span_rows)[:, None] >= jnp.arange(span_rows)[None, :]
    zero_level = jnp.zeros((heads_dev,), jnp.float32)
    carry_state = jnp.zeros((heads_dev, HEAD, STATE), jnp.float32)
    pieces = []
    for position in range(span_count):
        first_row = position * span_rows
        last_row = first_row + span_rows
        cum_block = cum_level[first_row:last_row]
        start_level = cum_level[first_row - 1] if position > 0 else zero_level
        scores = jnp.dot(
            output_state_map[first_row:last_row],
            input_state_map[first_row:last_row].T,
            preferred_element_type=jnp.float32,
        )
        weights = mixing(cum_block, scores, causal)
        weight_high, weight_low = split_parts(weights)
        x_span = act_heads[first_row:last_row]
        inner_part = jnp.einsum(
            "hts,shp->thp", weight_high, x_span, preferred_element_type=jnp.float32
        )
        inner_part = inner_part + jnp.einsum(
            "hts,shp->thp", weight_low, x_span, preferred_element_type=jnp.float32
        )
        inner_part = inner_part * input_scale[None, :, None]
        carried = jnp.exp(cum_block - start_level[None, :])[:, :, None] * jnp.einsum(
            "tn,hpn->thp", c_float[first_row:last_row], carry_state, precision=highest
        )
        pieces.append(inner_part + carried)
        end_level = cum_block[-1]
        tail_decay = jnp.exp(end_level[None, :] - cum_block)
        carry_state = jnp.exp(end_level - start_level)[:, None, None] * carry_state + jnp.einsum(
            "shp,sn->hpn",
            scaled[first_row:last_row] * tail_decay[:, :, None],
            b_float[first_row:last_row],
            precision=highest,
        )
    flat_state = carry_state.reshape(heads_dev, HEAD * STATE)
    level_lanes = jnp.broadcast_to(cum_level[-1][:, None], (heads_dev, 128))
    joined_all = lax.all_gather(jnp.concatenate([flat_state, level_lanes], axis=1), "seq")
    state_all = joined_all[:, :, : HEAD * STATE]
    level_all = joined_all[:, :, HEAD * STATE]
    incoming = carried_sum(state_all, level_all, seq_index, True)
    incoming = incoming.reshape(heads_dev, HEAD, STATE)
    outputs = jnp.concatenate(pieces, axis=0) + jnp.exp(cum_level)[:, :, None] * jnp.einsum(
        "tn,hpn->thp", c_float, incoming, precision=highest
    )
    mixed_out = (activations.astype(jnp.float32) + outputs.reshape(tokens, slice_width)).astype(
        jnp.bfloat16
    )
    g_rows, mixed_out = lax.optimization_barrier((g_rows, mixed_out))
    h_pick = jnp.einsum(
        "eb,brf->erf",
        chosen,
        mixed_out.reshape(blocks_dev, BLOCK, slice_width),
        preferred_element_type=jnp.float32,
    ).astype(jnp.bfloat16)
    h_block = dispatch(h_pick, exp_index, exp_count, mp_count, my_slice)
    h_all = lax.all_gather(h_block, "seq", axis=0)
    x_rows = compact(select, h_all, half_width)
    up_local = expert_up_weight[0]
    down_local = expert_down_weight[0]
    pre_act = mp_sum(jnp.dot(x_rows, up_local, preferred_element_type=jnp.float32))
    activation = jax.nn.silu(pre_act).astype(jnp.bfloat16)
    down_grad = jnp.einsum("tf,td->fd", activation, g_rows, preferred_element_type=jnp.float32)
    act_grad = mp_sum(
        jnp.einsum("td,fd->tf", g_rows, down_local, preferred_element_type=jnp.float32)
    )
    sigmoid_pre = jax.nn.sigmoid(pre_act)
    pre_grad = (act_grad * sigmoid_pre * (1.0 + pre_act * (1.0 - sigmoid_pre))).astype(jnp.bfloat16)
    up_grad = jnp.einsum("td,tf->df", x_rows, pre_grad, preferred_element_type=jnp.float32)
    shard_grad = spread(present, slot_of, pre_grad, pre_grad.shape[1])
    row_grad = jnp.einsum("tf,df->td", shard_grad, up_local, preferred_element_type=jnp.float32)
    spread_rows = row_grad.astype(jnp.bfloat16)
    back_rows = lax.psum_scatter(
        spread_rows,
        "seq",
        scatter_dimension=0,
        tiled=True,
    )
    returned = give_back(back_rows, exp_index, exp_count, mp_count)
    position = my_slice % exp_count
    chosen_by_shift = jnp.take(chosen, (position + jnp.arange(exp_count)) % exp_count, axis=0)
    token_grad = jnp.einsum(
        "kb,krf->brf", chosen_by_shift, returned, preferred_element_type=jnp.float32
    )
    total_grad = output_gradient.astype(jnp.float32) + token_grad.reshape(tokens, slice_width)
    grad_view = total_grad.reshape(tokens, heads_dev, HEAD)
    adjoint = jnp.zeros((heads_dev, HEAD, STATE), jnp.float32)
    back_pieces = [None] * span_count
    for position in reversed(range(span_count)):
        first_row = position * span_rows
        last_row = first_row + span_rows
        cum_block = cum_level[first_row:last_row]
        start_level = cum_level[first_row - 1] if position > 0 else zero_level
        scores = jnp.dot(
            output_state_map[first_row:last_row],
            input_state_map[first_row:last_row].T,
            preferred_element_type=jnp.float32,
        )
        weights = mixing(cum_block, scores, causal)
        weight_high, weight_low = split_parts(weights)
        grad_high, grad_low = split_parts(grad_view[first_row:last_row])
        inner_part = jnp.einsum(
            "hts,thp->shp", weight_high, grad_high, preferred_element_type=jnp.float32
        )
        inner_part = inner_part + jnp.einsum(
            "hts,thp->shp", weight_high, grad_low, preferred_element_type=jnp.float32
        )
        inner_part = inner_part + jnp.einsum(
            "hts,thp->shp", weight_low, grad_high, preferred_element_type=jnp.float32
        )
        end_level = cum_block[-1]
        tail_decay = jnp.exp(end_level[None, :] - cum_block)
        carried = tail_decay[:, :, None] * jnp.einsum(
            "sn,hpn->shp", b_float[first_row:last_row], adjoint, precision=highest
        )
        back_pieces[position] = inner_part + carried
        lead_decay = jnp.exp(cum_block - start_level[None, :])
        adjoint = jnp.exp(end_level - start_level)[:, None, None] * adjoint + jnp.einsum(
            "rhp,rn->hpn",
            grad_view[first_row:last_row] * lead_decay[:, :, None],
            c_float[first_row:last_row],
            precision=highest,
        )
    flat_adjoint = adjoint.reshape(heads_dev, HEAD * STATE)
    adjoint_all = lax.all_gather(flat_adjoint.astype(jnp.bfloat16), "seq")
    later_adjoint = carried_sum(adjoint_all, level_all, seq_index, False)
    later_adjoint = later_adjoint.reshape(heads_dev, HEAD, STATE)
    scan_grad = jnp.concatenate(back_pieces, axis=0) + jnp.exp(cum_level[-1][None, :] - cum_level)[
        :, :, None
    ] * jnp.einsum("sn,hpn->shp", b_float, later_adjoint, precision=highest)
    grad_x = total_grad + (input_scale[None, :, None] * scan_grad).reshape(tokens, slice_width)
    return (grad_x, up_grad[None], down_grad[None])


def solution(mesh):
    in_specs = (
        P("seq", ("expert", "mp")),
        P("seq", ("expert", "mp")),
        P("seq", None),
        P("seq", None),
        P(("expert", "mp")),
        P("seq"),
        P(),
        P("expert", "mp", "seq"),
        P("expert", "seq", "mp"),
    )
    out_specs = (P("seq", ("expert", "mp")), P("expert", "mp", "seq"), P("expert", "seq", "mp"))
    return jax.shard_map(
        per_device, mesh=mesh, in_specs=in_specs, out_specs=out_specs, check_vma=False
    )
```

```python
import jax
import jax.numpy as jnp
from jax import lax
from jax.sharding import PartitionSpec as P

HEAD = 64
STATE = 16
BLOCK = 128


spike_position_step = 0.3
highest = lax.Precision.HIGHEST


def carried_sum(values_all, level_all, own, earlier):
    count = level_all.shape[0]
    ids = jnp.arange(count)
    j, k = ids[:, None], ids[None, :]
    if earlier:
        between = (j < k) & (k < own)
        valid = ids < own
    else:
        between = (own < k) & (k < j)
        valid = ids > own
    exponent = jnp.sum(jnp.where(between[:, :, None], level_all[None], 0.0), axis=1)
    weight = jnp.where(valid[:, None], jnp.exp(exponent), 0.0)
    return jnp.sum(weight[:, :, None] * values_all.astype(jnp.float32), axis=0)


def mp_sum(part):
    part = part.astype(jnp.bfloat16)
    count = lax.axis_size("mp")
    total = part.astype(jnp.float32)
    for shift in range(1, count):
        pairs = [(src, (src + shift) % count) for src in range(count)]
        total = total + lax.ppermute(part, "mp", pairs).astype(jnp.float32)
    return total


def dispatch_pairs(exp_count, mp_count, shift):
    return [
        (src, ((src % exp_count + shift) % exp_count) * mp_count + src // exp_count)
        for src in range(exp_count * mp_count)
    ]


def dispatch(picks, exp_index, exp_count, mp_count, my_slice):
    position = my_slice % exp_count
    received = []
    for shift in range(exp_count):
        send = lax.dynamic_index_in_dim(picks, (position + shift) % exp_count, 0, keepdims=False)
        pairs = dispatch_pairs(exp_count, mp_count, shift)
        received.append(lax.ppermute(send, ("expert", "mp"), pairs))
    received = jnp.stack(received)
    order = (exp_index - jnp.arange(exp_count)) % exp_count
    placed = jnp.take(received, order, axis=0)
    rows, width = placed.shape[1], placed.shape[2]
    return placed.transpose(1, 0, 2).reshape(rows, exp_count * width)


def give_back(rows_half, exp_index, exp_count, mp_count):
    width = rows_half.shape[1] // exp_count
    pieces = rows_half.reshape(rows_half.shape[0], exp_count, width)
    received = []
    for shift in range(exp_count):
        column = (exp_index - shift) % exp_count
        send = lax.dynamic_index_in_dim(pieces, column, 1, keepdims=False)
        pairs = [(dst, src) for src, dst in dispatch_pairs(exp_count, mp_count, shift)]
        received.append(lax.ppermute(send, ("expert", "mp"), pairs))
    return jnp.stack(received)


def rounded(rounded_in):
    return lax.optimization_barrier(rounded_in.astype(jnp.bfloat16)).astype(jnp.float32)


def split_parts(values):
    high_part = values.astype(jnp.bfloat16)
    low_part = (values - high_part.astype(jnp.float32)).astype(jnp.bfloat16)
    return (high_part, low_part)


def mixing(cum_block, scores, causal):
    spread = cum_block.T[:, :, None] - cum_block.T[:, None, :]
    spread = jnp.where(causal[None], spread, -jnp.inf)
    return jnp.exp(spread) * scores[None]


def compact(select, gathered, half_width):
    blocks = gathered.reshape(select.shape[1], -1, half_width)
    used = jnp.any(select > 0, axis=1)
    source = jnp.argmax(select, axis=1)
    rows_out = jnp.where(used[:, None, None], jnp.take(blocks, source, axis=0, mode="clip"), 0)
    return rows_out.reshape(-1, half_width).astype(jnp.bfloat16)


def spread(present, slot_of, rows, half_width):
    blocks = rows.reshape(-1, BLOCK, half_width)
    placed = jnp.take(blocks, jnp.maximum(slot_of, 0), axis=0, mode="clip")
    placed = jnp.where(present[:, None, None], placed, 0)
    return placed.reshape(-1, half_width).astype(jnp.bfloat16)


def per_device(
    activations,
    output_gradient,
    input_state_map,
    output_state_map,
    head_decay_speed,
    spike_decay_level,
    assign,
    expert_up_weight,
    expert_down_weight,
):
    tokens, slice_width = activations.shape
    heads_dev = slice_width // HEAD
    seq_count = lax.axis_size("seq")
    exp_count = lax.axis_size("expert")
    mp_count = lax.axis_size("mp")
    seq_index = lax.axis_index("seq")
    exp_index = lax.axis_index("expert")
    mp_index = lax.axis_index("mp")
    my_slice = exp_index * mp_count + mp_index
    half_width = slice_width * exp_count
    slot_total = seq_count // 2
    blocks_dev = tokens // BLOCK
    route_table = assign.reshape(seq_count, blocks_dev)
    own_row = lax.dynamic_index_in_dim(route_table, seq_index, 0, keepdims=False)
    chosen = (own_row[None, :] == jnp.arange(exp_count)[:, None]).astype(jnp.bfloat16)
    g_pick = jnp.einsum(
        "eb,brf->erf",
        chosen,
        output_gradient.reshape(blocks_dev, BLOCK, slice_width),
        preferred_element_type=jnp.float32,
    ).astype(jnp.bfloat16)
    g_block = dispatch(g_pick, exp_index, exp_count, mp_count, my_slice)
    g_all = lax.all_gather(g_block, "seq", axis=0)
    present = jnp.any(route_table == exp_index, axis=1)
    slot_of = jnp.cumsum(present.astype(jnp.int32)) - 1
    select = ((slot_of[None, :] == jnp.arange(slot_total)[:, None]) & present[None, :]).astype(
        jnp.bfloat16
    )
    g_rows = compact(select, g_all, half_width)
    input_scale = jnp.sqrt(1.0 - jnp.exp(-2.0 * head_decay_speed))
    cum_level = jnp.cumsum(
        -head_decay_speed[None, :]
        - spike_position_step * spike_decay_level.astype(jnp.float32)[:, None],
        axis=0,
    )
    b_float = input_state_map.astype(jnp.float32)
    c_float = output_state_map.astype(jnp.float32)
    act_heads = activations.reshape(tokens, heads_dev, HEAD)
    scaled = act_heads.astype(jnp.float32) * input_scale[None, :, None]
    span_rows = min(512, tokens)
    span_count = tokens // span_rows
    causal = jnp.arange(span_rows)[:, None] >= jnp.arange(span_rows)[None, :]
    zero_level = jnp.zeros((heads_dev,), jnp.float32)
    carry_state = jnp.zeros((heads_dev, HEAD, STATE), jnp.float32)
    pieces = []
    for position in range(span_count):
        first_row = position * span_rows
        last_row = first_row + span_rows
        cum_block = cum_level[first_row:last_row]
        start_level = cum_level[first_row - 1] if position > 0 else zero_level
        scores = jnp.dot(
            output_state_map[first_row:last_row],
            input_state_map[first_row:last_row].T,
            preferred_element_type=jnp.float32,
        )
        weights = mixing(cum_block, scores, causal)
        weight_high, weight_low = split_parts(weights)
        x_span = act_heads[first_row:last_row]
        inner_part = jnp.einsum(
            "hts,shp->thp", weight_high, x_span, preferred_element_type=jnp.float32
        )
        inner_part = inner_part + jnp.einsum(
            "hts,shp->thp", weight_low, x_span, preferred_element_type=jnp.float32
        )
        inner_part = inner_part * input_scale[None, :, None]
        carried = jnp.exp(cum_block - start_level[None, :])[:, :, None] * jnp.einsum(
            "tn,hpn->thp", c_float[first_row:last_row], carry_state, precision=highest
        )
        pieces.append(inner_part + carried)
        end_level = cum_block[-1]
        tail_decay = jnp.exp(end_level[None, :] - cum_block)
        carry_state = jnp.exp(end_level - start_level)[:, None, None] * carry_state + jnp.einsum(
            "shp,sn->hpn",
            scaled[first_row:last_row] * tail_decay[:, :, None],
            b_float[first_row:last_row],
            precision=highest,
        )
    flat_state = carry_state.reshape(heads_dev, HEAD * STATE)
    level_lanes = jnp.broadcast_to(cum_level[-1][:, None], (heads_dev, 128))
    joined_all = lax.all_gather(jnp.concatenate([flat_state, level_lanes], axis=1), "seq")
    state_all = joined_all[:, :, : HEAD * STATE]
    level_all = joined_all[:, :, HEAD * STATE]
    incoming = carried_sum(state_all, level_all, seq_index, True)
    incoming = incoming.reshape(heads_dev, HEAD, STATE)
    outputs = jnp.concatenate(pieces, axis=0) + jnp.exp(cum_level)[:, :, None] * jnp.einsum(
        "tn,hpn->thp", c_float, incoming, precision=highest
    )
    mixed_out = (activations.astype(jnp.float32) + outputs.reshape(tokens, slice_width)).astype(
        jnp.bfloat16
    )
    g_rows, mixed_out = lax.optimization_barrier((g_rows, mixed_out))
    h_pick = jnp.einsum(
        "eb,brf->erf",
        chosen,
        mixed_out.reshape(blocks_dev, BLOCK, slice_width),
        preferred_element_type=jnp.float32,
    ).astype(jnp.bfloat16)
    h_block = dispatch(h_pick, exp_index, exp_count, mp_count, my_slice)
    h_all = lax.all_gather(h_block, "seq", axis=0)
    x_rows = compact(select, h_all, half_width)
    up_local = expert_up_weight[0]
    down_local = expert_down_weight[0]
    pre_act = mp_sum(jnp.dot(x_rows, up_local, preferred_element_type=jnp.float32))
    activation = jax.nn.silu(pre_act).astype(jnp.bfloat16)
    down_grad = jnp.einsum("tf,td->fd", activation, g_rows, preferred_element_type=jnp.float32)
    act_grad = mp_sum(
        jnp.einsum("td,fd->tf", g_rows, down_local, preferred_element_type=jnp.float32)
    )
    sigmoid_pre = jax.nn.sigmoid(pre_act)
    pre_grad = (act_grad * sigmoid_pre * (1.0 + pre_act * (1.0 - sigmoid_pre))).astype(jnp.bfloat16)
    up_grad = jnp.einsum("td,tf->df", x_rows, pre_grad, preferred_element_type=jnp.float32)
    shard_grad = spread(present, slot_of, pre_grad, pre_grad.shape[1])
    row_grad = jnp.einsum("tf,df->td", shard_grad, up_local, preferred_element_type=jnp.float32)
    spread_rows = row_grad.astype(jnp.bfloat16)
    back_rows = lax.psum_scatter(
        spread_rows,
        "seq",
        scatter_dimension=0,
        tiled=True,
    )
    up_grad, down_grad, back_rows = lax.optimization_barrier((up_grad, down_grad, back_rows))
    returned = give_back(back_rows, exp_index, exp_count, mp_count)
    position = my_slice % exp_count
    chosen_by_shift = jnp.take(chosen, (position + jnp.arange(exp_count)) % exp_count, axis=0)
    token_grad = jnp.einsum(
        "kb,krf->brf", chosen_by_shift, returned, preferred_element_type=jnp.float32
    )
    total_grad = output_gradient.astype(jnp.float32) + token_grad.reshape(tokens, slice_width)
    grad_view = total_grad.reshape(tokens, heads_dev, HEAD)
    adjoint = jnp.zeros((heads_dev, HEAD, STATE), jnp.float32)
    back_pieces = [None] * span_count
    for position in reversed(range(span_count)):
        first_row = position * span_rows
        last_row = first_row + span_rows
        cum_block = cum_level[first_row:last_row]
        start_level = cum_level[first_row - 1] if position > 0 else zero_level
        scores = jnp.dot(
            output_state_map[first_row:last_row],
            input_state_map[first_row:last_row].T,
            preferred_element_type=jnp.float32,
        )
        weights = mixing(cum_block, scores, causal)
        weight_high, weight_low = split_parts(weights)
        grad_high, grad_low = split_parts(grad_view[first_row:last_row])
        inner_part = jnp.einsum(
            "hts,thp->shp", weight_high, grad_high, preferred_element_type=jnp.float32
        )
        inner_part = inner_part + jnp.einsum(
            "hts,thp->shp", weight_high, grad_low, preferred_element_type=jnp.float32
        )
        inner_part = inner_part + jnp.einsum(
            "hts,thp->shp", weight_low, grad_high, preferred_element_type=jnp.float32
        )
        end_level = cum_block[-1]
        tail_decay = jnp.exp(end_level[None, :] - cum_block)
        carried = tail_decay[:, :, None] * jnp.einsum(
            "sn,hpn->shp", b_float[first_row:last_row], adjoint, precision=highest
        )
        back_pieces[position] = inner_part + carried
        lead_decay = jnp.exp(cum_block - start_level[None, :])
        adjoint = jnp.exp(end_level - start_level)[:, None, None] * adjoint + jnp.einsum(
            "rhp,rn->hpn",
            grad_view[first_row:last_row] * lead_decay[:, :, None],
            c_float[first_row:last_row],
            precision=highest,
        )
    flat_adjoint = adjoint.reshape(heads_dev, HEAD * STATE)
    adjoint_all = lax.all_gather(flat_adjoint.astype(jnp.bfloat16), "seq")
    later_adjoint = carried_sum(adjoint_all, level_all, seq_index, False)
    later_adjoint = later_adjoint.reshape(heads_dev, HEAD, STATE)
    scan_grad = jnp.concatenate(back_pieces, axis=0) + jnp.exp(cum_level[-1][None, :] - cum_level)[
        :, :, None
    ] * jnp.einsum("sn,hpn->shp", b_float, later_adjoint, precision=highest)
    grad_x = total_grad + (input_scale[None, :, None] * scan_grad).reshape(tokens, slice_width)
    return (grad_x, up_grad[None], down_grad[None])


def solution(mesh):
    in_specs = (
        P("seq", ("expert", "mp")),
        P("seq", ("expert", "mp")),
        P("seq", None),
        P("seq", None),
        P(("expert", "mp")),
        P("seq"),
        P(),
        P("expert", "mp", "seq"),
        P("expert", "seq", "mp"),
    )
    out_specs = (P("seq", ("expert", "mp")), P("expert", "mp", "seq"), P("expert", "seq", "mp"))
    return jax.shard_map(
        per_device, mesh=mesh, in_specs=in_specs, out_specs=out_specs, check_vma=False
    )
```

```python
import jax
import jax.numpy as jnp
from jax import lax
from jax.sharding import PartitionSpec as P

HEAD = 64
STATE = 16
BLOCK = 128


spike_position_step = 0.3
highest = lax.Precision.HIGHEST


def carried_sum(values_all, level_all, own, earlier):
    count = level_all.shape[0]
    ids = jnp.arange(count)
    j, k = ids[:, None], ids[None, :]
    if earlier:
        between = (j < k) & (k < own)
        valid = ids < own
    else:
        between = (own < k) & (k < j)
        valid = ids > own
    exponent = jnp.sum(jnp.where(between[:, :, None], level_all[None], 0.0), axis=1)
    weight = jnp.where(valid[:, None], jnp.exp(exponent), 0.0)
    return jnp.sum(weight[:, :, None] * values_all.astype(jnp.float32), axis=0)


def mp_sum(part):
    part = part.astype(jnp.bfloat16)
    count = lax.axis_size("mp")
    total = part.astype(jnp.float32)
    for shift in range(1, count):
        pairs = [(src, (src + shift) % count) for src in range(count)]
        total = total + lax.ppermute(part, "mp", pairs).astype(jnp.float32)
    return total


def dispatch_pairs(exp_count, mp_count, shift):
    return [
        (src, ((src % exp_count + shift) % exp_count) * mp_count + src // exp_count)
        for src in range(exp_count * mp_count)
    ]


def dispatch(picks, exp_index, exp_count, mp_count, my_slice):
    position = my_slice % exp_count
    received = []
    for shift in range(exp_count):
        send = lax.dynamic_index_in_dim(picks, (position + shift) % exp_count, 0, keepdims=False)
        pairs = dispatch_pairs(exp_count, mp_count, shift)
        received.append(lax.ppermute(send, ("expert", "mp"), pairs))
    received = jnp.stack(received)
    order = (exp_index - jnp.arange(exp_count)) % exp_count
    placed = jnp.take(received, order, axis=0)
    rows, width = placed.shape[1], placed.shape[2]
    return placed.transpose(1, 0, 2).reshape(rows, exp_count * width)


def give_back(rows_half, exp_index, exp_count, mp_count):
    width = rows_half.shape[1] // exp_count
    pieces = rows_half.reshape(rows_half.shape[0], exp_count, width)
    received = []
    for shift in range(exp_count):
        column = (exp_index - shift) % exp_count
        send = lax.dynamic_index_in_dim(pieces, column, 1, keepdims=False)
        pairs = [(dst, src) for src, dst in dispatch_pairs(exp_count, mp_count, shift)]
        received.append(lax.ppermute(send, ("expert", "mp"), pairs))
    return jnp.stack(received)


def rounded(rounded_in):
    return lax.optimization_barrier(rounded_in.astype(jnp.bfloat16)).astype(jnp.float32)


def split_parts(values):
    high_part = values.astype(jnp.bfloat16)
    low_part = (values - high_part.astype(jnp.float32)).astype(jnp.bfloat16)
    return (high_part, low_part)


def mixing(cum_block, scores, causal):
    spread = cum_block.T[:, :, None] - cum_block.T[:, None, :]
    spread = jnp.where(causal[None], spread, -jnp.inf)
    return jnp.exp(spread) * scores[None]


def compact(select, gathered, half_width):
    blocks = gathered.reshape(select.shape[1], -1, half_width)
    used = jnp.any(select > 0, axis=1)
    source = jnp.argmax(select, axis=1)
    rows_out = jnp.where(used[:, None, None], jnp.take(blocks, source, axis=0, mode="clip"), 0)
    return rows_out.reshape(-1, half_width).astype(jnp.bfloat16)


def spread(present, slot_of, rows, half_width):
    blocks = rows.reshape(-1, BLOCK, half_width)
    placed = jnp.take(blocks, jnp.maximum(slot_of, 0), axis=0, mode="clip")
    placed = jnp.where(present[:, None, None], placed, 0)
    return placed.reshape(-1, half_width).astype(jnp.bfloat16)


def per_device(
    activations,
    output_gradient,
    input_state_map,
    output_state_map,
    head_decay_speed,
    spike_decay_level,
    assign,
    expert_up_weight,
    expert_down_weight,
):
    tokens, slice_width = activations.shape
    heads_dev = slice_width // HEAD
    seq_count = lax.axis_size("seq")
    exp_count = lax.axis_size("expert")
    mp_count = lax.axis_size("mp")
    seq_index = lax.axis_index("seq")
    exp_index = lax.axis_index("expert")
    mp_index = lax.axis_index("mp")
    my_slice = exp_index * mp_count + mp_index
    half_width = slice_width * exp_count
    slot_total = seq_count // 2
    blocks_dev = tokens // BLOCK
    route_table = assign.reshape(seq_count, blocks_dev)
    own_row = lax.dynamic_index_in_dim(route_table, seq_index, 0, keepdims=False)
    chosen = (own_row[None, :] == jnp.arange(exp_count)[:, None]).astype(jnp.bfloat16)
    g_pick = jnp.einsum(
        "eb,brf->erf",
        chosen,
        output_gradient.reshape(blocks_dev, BLOCK, slice_width),
        preferred_element_type=jnp.float32,
    ).astype(jnp.bfloat16)
    g_block = dispatch(g_pick, exp_index, exp_count, mp_count, my_slice)
    g_all = lax.all_gather(g_block, "seq", axis=0)
    present = jnp.any(route_table == exp_index, axis=1)
    slot_of = jnp.cumsum(present.astype(jnp.int32)) - 1
    select = ((slot_of[None, :] == jnp.arange(slot_total)[:, None]) & present[None, :]).astype(
        jnp.bfloat16
    )
    input_scale = jnp.sqrt(1.0 - jnp.exp(-2.0 * head_decay_speed))
    cum_level = jnp.cumsum(
        -head_decay_speed[None, :]
        - spike_position_step * spike_decay_level.astype(jnp.float32)[:, None],
        axis=0,
    )
    b_float = input_state_map.astype(jnp.float32)
    c_float = output_state_map.astype(jnp.float32)
    act_heads = activations.reshape(tokens, heads_dev, HEAD)
    scaled = act_heads.astype(jnp.float32) * input_scale[None, :, None]
    span_rows = min(512, tokens)
    span_count = tokens // span_rows
    causal = jnp.arange(span_rows)[:, None] >= jnp.arange(span_rows)[None, :]
    zero_level = jnp.zeros((heads_dev,), jnp.float32)
    carry_state = jnp.zeros((heads_dev, HEAD, STATE), jnp.float32)
    pieces = []
    for position in range(span_count):
        first_row = position * span_rows
        last_row = first_row + span_rows
        cum_block = cum_level[first_row:last_row]
        start_level = cum_level[first_row - 1] if position > 0 else zero_level
        scores = jnp.dot(
            output_state_map[first_row:last_row],
            input_state_map[first_row:last_row].T,
            preferred_element_type=jnp.float32,
        )
        weights = mixing(cum_block, scores, causal)
        weight_high, weight_low = split_parts(weights)
        x_span = act_heads[first_row:last_row]
        inner_part = jnp.einsum(
            "hts,shp->thp", weight_high, x_span, preferred_element_type=jnp.float32
        )
        inner_part = inner_part + jnp.einsum(
            "hts,shp->thp", weight_low, x_span, preferred_element_type=jnp.float32
        )
        inner_part = inner_part * input_scale[None, :, None]
        carried = jnp.exp(cum_block - start_level[None, :])[:, :, None] * jnp.einsum(
            "tn,hpn->thp", c_float[first_row:last_row], carry_state, precision=highest
        )
        pieces.append(inner_part + carried)
        end_level = cum_block[-1]
        tail_decay = jnp.exp(end_level[None, :] - cum_block)
        carry_state = jnp.exp(end_level - start_level)[:, None, None] * carry_state + jnp.einsum(
            "shp,sn->hpn",
            scaled[first_row:last_row] * tail_decay[:, :, None],
            b_float[first_row:last_row],
            precision=highest,
        )
    flat_state = carry_state.reshape(heads_dev, HEAD * STATE)
    level_lanes = jnp.broadcast_to(cum_level[-1][:, None], (heads_dev, 128))
    joined_all = lax.all_gather(jnp.concatenate([flat_state, level_lanes], axis=1), "seq")
    state_all = joined_all[:, :, : HEAD * STATE]
    level_all = joined_all[:, :, HEAD * STATE]
    incoming = carried_sum(state_all, level_all, seq_index, True)
    incoming = incoming.reshape(heads_dev, HEAD, STATE)
    outputs = jnp.concatenate(pieces, axis=0) + jnp.exp(cum_level)[:, :, None] * jnp.einsum(
        "tn,hpn->thp", c_float, incoming, precision=highest
    )
    mixed_out = (activations.astype(jnp.float32) + outputs.reshape(tokens, slice_width)).astype(
        jnp.bfloat16
    )
    g_all, mixed_out = lax.optimization_barrier((g_all, mixed_out))
    h_pick = jnp.einsum(
        "eb,brf->erf",
        chosen,
        mixed_out.reshape(blocks_dev, BLOCK, slice_width),
        preferred_element_type=jnp.float32,
    ).astype(jnp.bfloat16)
    h_block = dispatch(h_pick, exp_index, exp_count, mp_count, my_slice)
    h_all = lax.all_gather(h_block, "seq", axis=0)
    g_rows = compact(select, g_all, half_width)
    down_local = expert_down_weight[0]
    act_grad = mp_sum(
        jnp.einsum("td,fd->tf", g_rows, down_local, preferred_element_type=jnp.float32)
    )
    g_rows, act_grad, h_all = lax.optimization_barrier((g_rows, act_grad, h_all))
    x_rows = compact(select, h_all, half_width)
    up_local = expert_up_weight[0]
    pre_act = mp_sum(jnp.dot(x_rows, up_local, preferred_element_type=jnp.float32))
    activation = jax.nn.silu(pre_act).astype(jnp.bfloat16)
    down_grad = jnp.einsum("tf,td->fd", activation, g_rows, preferred_element_type=jnp.float32)
    sigmoid_pre = jax.nn.sigmoid(pre_act)
    pre_grad = (act_grad * sigmoid_pre * (1.0 + pre_act * (1.0 - sigmoid_pre))).astype(jnp.bfloat16)
    up_grad = jnp.einsum("td,tf->df", x_rows, pre_grad, preferred_element_type=jnp.float32)
    shard_grad = spread(present, slot_of, pre_grad, pre_grad.shape[1])
    row_grad = jnp.einsum("tf,df->td", shard_grad, up_local, preferred_element_type=jnp.float32)
    spread_rows = row_grad.astype(jnp.bfloat16)
    back_rows = lax.psum_scatter(
        spread_rows,
        "seq",
        scatter_dimension=0,
        tiled=True,
    )
    up_grad, down_grad, back_rows = lax.optimization_barrier((up_grad, down_grad, back_rows))
    returned = give_back(back_rows, exp_index, exp_count, mp_count)
    position = my_slice % exp_count
    chosen_by_shift = jnp.take(chosen, (position + jnp.arange(exp_count)) % exp_count, axis=0)
    token_grad = jnp.einsum(
        "kb,krf->brf", chosen_by_shift, returned, preferred_element_type=jnp.float32
    )
    total_grad = output_gradient.astype(jnp.float32) + token_grad.reshape(tokens, slice_width)
    grad_view = total_grad.reshape(tokens, heads_dev, HEAD)
    adjoint = jnp.zeros((heads_dev, HEAD, STATE), jnp.float32)
    back_pieces = [None] * span_count
    for position in reversed(range(span_count)):
        first_row = position * span_rows
        last_row = first_row + span_rows
        cum_block = cum_level[first_row:last_row]
        start_level = cum_level[first_row - 1] if position > 0 else zero_level
        scores = jnp.dot(
            output_state_map[first_row:last_row],
            input_state_map[first_row:last_row].T,
            preferred_element_type=jnp.float32,
        )
        weights = mixing(cum_block, scores, causal)
        weight_high, weight_low = split_parts(weights)
        grad_high, grad_low = split_parts(grad_view[first_row:last_row])
        inner_part = jnp.einsum(
            "hts,thp->shp", weight_high, grad_high, preferred_element_type=jnp.float32
        )
        inner_part = inner_part + jnp.einsum(
            "hts,thp->shp", weight_high, grad_low, preferred_element_type=jnp.float32
        )
        inner_part = inner_part + jnp.einsum(
            "hts,thp->shp", weight_low, grad_high, preferred_element_type=jnp.float32
        )
        end_level = cum_block[-1]
        tail_decay = jnp.exp(end_level[None, :] - cum_block)
        carried = tail_decay[:, :, None] * jnp.einsum(
            "sn,hpn->shp", b_float[first_row:last_row], adjoint, precision=highest
        )
        back_pieces[position] = inner_part + carried
        lead_decay = jnp.exp(cum_block - start_level[None, :])
        adjoint = jnp.exp(end_level - start_level)[:, None, None] * adjoint + jnp.einsum(
            "rhp,rn->hpn",
            grad_view[first_row:last_row] * lead_decay[:, :, None],
            c_float[first_row:last_row],
            precision=highest,
        )
    flat_adjoint = adjoint.reshape(heads_dev, HEAD * STATE)
    adjoint_all = lax.all_gather(flat_adjoint.astype(jnp.bfloat16), "seq")
    later_adjoint = carried_sum(adjoint_all, level_all, seq_index, False)
    later_adjoint = later_adjoint.reshape(heads_dev, HEAD, STATE)
    scan_grad = jnp.concatenate(back_pieces, axis=0) + jnp.exp(cum_level[-1][None, :] - cum_level)[
        :, :, None
    ] * jnp.einsum("sn,hpn->shp", b_float, later_adjoint, precision=highest)
    grad_x = total_grad + (input_scale[None, :, None] * scan_grad).reshape(tokens, slice_width)
    return (grad_x, up_grad[None], down_grad[None])


def solution(mesh):
    in_specs = (
        P("seq", ("expert", "mp")),
        P("seq", ("expert", "mp")),
        P("seq", None),
        P("seq", None),
        P(("expert", "mp")),
        P("seq"),
        P(),
        P("expert", "mp", "seq"),
        P("expert", "seq", "mp"),
    )
    out_specs = (P("seq", ("expert", "mp")), P("expert", "mp", "seq"), P("expert", "seq", "mp"))
    return jax.shard_map(
        per_device, mesh=mesh, in_specs=in_specs, out_specs=out_specs, check_vma=False
    )
```

```python
import jax
import jax.numpy as jnp
from jax import lax
from jax.sharding import PartitionSpec as P

HEAD = 64
STATE = 16
BLOCK = 128


spike_position_step = 0.3
highest = lax.Precision.HIGHEST


def carried_sum(values_all, level_all, own, earlier):
    count = level_all.shape[0]
    ids = jnp.arange(count)
    j, k = ids[:, None], ids[None, :]
    if earlier:
        between = (j < k) & (k < own)
        valid = ids < own
    else:
        between = (own < k) & (k < j)
        valid = ids > own
    exponent = jnp.sum(jnp.where(between[:, :, None], level_all[None], 0.0), axis=1)
    weight = jnp.where(valid[:, None], jnp.exp(exponent), 0.0)
    return jnp.sum(weight[:, :, None] * values_all.astype(jnp.float32), axis=0)


def torus_gather(value, count):
    side = 4
    if count != side * side:
        return lax.all_gather(value, "seq")
    own = lax.axis_index("seq")
    row, col = own // side, own % side
    steps = jnp.arange(side)
    got = [value]
    for shift in range(1, side):
        pairs = [(r * side + c, r * side + (c + shift) % side) for r in range(side) for c in range(side)]
        got.append(lax.ppermute(value, "seq", pairs))
    line = jnp.take(jnp.stack(got), (col - steps) % side, axis=0)
    got = [line]
    for shift in range(1, side):
        pairs = [(r * side + c, ((r + shift) % side) * side + c) for r in range(side) for c in range(side)]
        got.append(lax.ppermute(line, "seq", pairs))
    whole = jnp.take(jnp.stack(got), (row - steps) % side, axis=0)
    return whole.reshape((count,) + value.shape)


def mp_sum(part):
    part = part.astype(jnp.bfloat16)
    count = lax.axis_size("mp")
    total = part.astype(jnp.float32)
    for shift in range(1, count):
        pairs = [(src, (src + shift) % count) for src in range(count)]
        total = total + lax.ppermute(part, "mp", pairs).astype(jnp.float32)
    return total


def dispatch_pairs(exp_count, mp_count, shift):
    return [
        (src, ((src % exp_count + shift) % exp_count) * mp_count + src // exp_count)
        for src in range(exp_count * mp_count)
    ]


def dispatch(picks, exp_index, exp_count, mp_count, my_slice):
    position = my_slice % exp_count
    received = []
    for shift in range(exp_count):
        send = lax.dynamic_index_in_dim(picks, (position + shift) % exp_count, 0, keepdims=False)
        pairs = dispatch_pairs(exp_count, mp_count, shift)
        received.append(lax.ppermute(send, ("expert", "mp"), pairs))
    received = jnp.stack(received)
    order = (exp_index - jnp.arange(exp_count)) % exp_count
    placed = jnp.take(received, order, axis=0)
    rows, width = placed.shape[1], placed.shape[2]
    return placed.transpose(1, 0, 2).reshape(rows, exp_count * width)


def give_back(rows_half, exp_index, exp_count, mp_count):
    width = rows_half.shape[1] // exp_count
    pieces = rows_half.reshape(rows_half.shape[0], exp_count, width)
    received = []
    for shift in range(exp_count):
        column = (exp_index - shift) % exp_count
        send = lax.dynamic_index_in_dim(pieces, column, 1, keepdims=False)
        pairs = [(dst, src) for src, dst in dispatch_pairs(exp_count, mp_count, shift)]
        received.append(lax.ppermute(send, ("expert", "mp"), pairs))
    return jnp.stack(received)


def rounded(rounded_in):
    return lax.optimization_barrier(rounded_in.astype(jnp.bfloat16)).astype(jnp.float32)


def split_parts(values):
    high_part = values.astype(jnp.bfloat16)
    low_part = (values - high_part.astype(jnp.float32)).astype(jnp.bfloat16)
    return (high_part, low_part)


def mixing(cum_block, scores, causal):
    spread = cum_block.T[:, :, None] - cum_block.T[:, None, :]
    spread = jnp.where(causal[None], spread, -jnp.inf)
    return jnp.exp(spread) * scores[None]


def compact(select, gathered, half_width):
    blocks = gathered.reshape(select.shape[1], -1, half_width)
    used = jnp.any(select > 0, axis=1)
    source = jnp.argmax(select, axis=1)
    rows_out = jnp.where(used[:, None, None], jnp.take(blocks, source, axis=0, mode="clip"), 0)
    return rows_out.reshape(-1, half_width).astype(jnp.bfloat16)


def spread(present, slot_of, rows, half_width):
    blocks = rows.reshape(-1, BLOCK, half_width)
    placed = jnp.take(blocks, jnp.maximum(slot_of, 0), axis=0, mode="clip")
    placed = jnp.where(present[:, None, None], placed, 0)
    return placed.reshape(-1, half_width).astype(jnp.bfloat16)


def per_device(
    activations,
    output_gradient,
    input_state_map,
    output_state_map,
    head_decay_speed,
    spike_decay_level,
    assign,
    expert_up_weight,
    expert_down_weight,
):
    tokens, slice_width = activations.shape
    heads_dev = slice_width // HEAD
    seq_count = lax.axis_size("seq")
    exp_count = lax.axis_size("expert")
    mp_count = lax.axis_size("mp")
    seq_index = lax.axis_index("seq")
    exp_index = lax.axis_index("expert")
    mp_index = lax.axis_index("mp")
    my_slice = exp_index * mp_count + mp_index
    half_width = slice_width * exp_count
    slot_total = seq_count // 2
    blocks_dev = tokens // BLOCK
    route_table = assign.reshape(seq_count, blocks_dev)
    own_row = lax.dynamic_index_in_dim(route_table, seq_index, 0, keepdims=False)
    chosen = (own_row[None, :] == jnp.arange(exp_count)[:, None]).astype(jnp.bfloat16)
    g_pick = jnp.einsum(
        "eb,brf->erf",
        chosen,
        output_gradient.reshape(blocks_dev, BLOCK, slice_width),
        preferred_element_type=jnp.float32,
    ).astype(jnp.bfloat16)
    g_block = dispatch(g_pick, exp_index, exp_count, mp_count, my_slice)
    g_all = lax.all_gather(g_block, "seq", axis=0)
    present = jnp.any(route_table == exp_index, axis=1)
    slot_of = jnp.cumsum(present.astype(jnp.int32)) - 1
    select = ((slot_of[None, :] == jnp.arange(slot_total)[:, None]) & present[None, :]).astype(
        jnp.bfloat16
    )
    input_scale = jnp.sqrt(1.0 - jnp.exp(-2.0 * head_decay_speed))
    cum_level = jnp.cumsum(
        -head_decay_speed[None, :]
        - spike_position_step * spike_decay_level.astype(jnp.float32)[:, None],
        axis=0,
    )
    b_float = input_state_map.astype(jnp.float32)
    c_float = output_state_map.astype(jnp.float32)
    act_heads = activations.reshape(tokens, heads_dev, HEAD)
    scaled = act_heads.astype(jnp.float32) * input_scale[None, :, None]
    span_rows = min(512, tokens)
    span_count = tokens // span_rows
    causal = jnp.arange(span_rows)[:, None] >= jnp.arange(span_rows)[None, :]
    zero_level = jnp.zeros((heads_dev,), jnp.float32)
    carry_state = jnp.zeros((heads_dev, HEAD, STATE), jnp.float32)
    pieces = []
    for position in range(span_count):
        first_row = position * span_rows
        last_row = first_row + span_rows
        cum_block = cum_level[first_row:last_row]
        start_level = cum_level[first_row - 1] if position > 0 else zero_level
        scores = jnp.dot(
            output_state_map[first_row:last_row],
            input_state_map[first_row:last_row].T,
            preferred_element_type=jnp.float32,
        )
        weights = mixing(cum_block, scores, causal)
        weight_high, weight_low = split_parts(weights)
        x_span = act_heads[first_row:last_row]
        inner_part = jnp.einsum(
            "hts,shp->thp", weight_high, x_span, preferred_element_type=jnp.float32
        )
        inner_part = inner_part + jnp.einsum(
            "hts,shp->thp", weight_low, x_span, preferred_element_type=jnp.float32
        )
        inner_part = inner_part * input_scale[None, :, None]
        carried = jnp.exp(cum_block - start_level[None, :])[:, :, None] * jnp.einsum(
            "tn,hpn->thp", c_float[first_row:last_row], carry_state, precision=highest
        )
        pieces.append(inner_part + carried)
        end_level = cum_block[-1]
        tail_decay = jnp.exp(end_level[None, :] - cum_block)
        carry_state = jnp.exp(end_level - start_level)[:, None, None] * carry_state + jnp.einsum(
            "shp,sn->hpn",
            scaled[first_row:last_row] * tail_decay[:, :, None],
            b_float[first_row:last_row],
            precision=highest,
        )
    flat_state = carry_state.reshape(heads_dev, HEAD * STATE)
    level_lanes = jnp.broadcast_to(cum_level[-1][:, None], (heads_dev, 128))
    joined_all = lax.all_gather(jnp.concatenate([flat_state, level_lanes], axis=1), "seq")
    state_all = joined_all[:, :, : HEAD * STATE]
    level_all = joined_all[:, :, HEAD * STATE]
    incoming = carried_sum(state_all, level_all, seq_index, True)
    incoming = incoming.reshape(heads_dev, HEAD, STATE)
    outputs = jnp.concatenate(pieces, axis=0) + jnp.exp(cum_level)[:, :, None] * jnp.einsum(
        "tn,hpn->thp", c_float, incoming, precision=highest
    )
    mixed_out = (activations.astype(jnp.float32) + outputs.reshape(tokens, slice_width)).astype(
        jnp.bfloat16
    )
    g_all, mixed_out = lax.optimization_barrier((g_all, mixed_out))
    h_pick = jnp.einsum(
        "eb,brf->erf",
        chosen,
        mixed_out.reshape(blocks_dev, BLOCK, slice_width),
        preferred_element_type=jnp.float32,
    ).astype(jnp.bfloat16)
    h_block = dispatch(h_pick, exp_index, exp_count, mp_count, my_slice)
    h_all = lax.all_gather(h_block, "seq", axis=0)
    g_rows = compact(select, g_all, half_width)
    down_local = expert_down_weight[0]
    act_grad = mp_sum(
        jnp.einsum("td,fd->tf", g_rows, down_local, preferred_element_type=jnp.float32)
    )
    g_rows, act_grad, h_all = lax.optimization_barrier((g_rows, act_grad, h_all))
    x_rows = compact(select, h_all, half_width)
    up_local = expert_up_weight[0]
    pre_act = mp_sum(jnp.dot(x_rows, up_local, preferred_element_type=jnp.float32))
    activation = jax.nn.silu(pre_act).astype(jnp.bfloat16)
    down_grad = jnp.einsum("tf,td->fd", activation, g_rows, preferred_element_type=jnp.float32)
    sigmoid_pre = jax.nn.sigmoid(pre_act)
    pre_grad = (act_grad * sigmoid_pre * (1.0 + pre_act * (1.0 - sigmoid_pre))).astype(jnp.bfloat16)
    up_grad = jnp.einsum("td,tf->df", x_rows, pre_grad, preferred_element_type=jnp.float32)
    shard_grad = spread(present, slot_of, pre_grad, pre_grad.shape[1])
    row_grad = jnp.einsum("tf,df->td", shard_grad, up_local, preferred_element_type=jnp.float32)
    spread_rows = row_grad.astype(jnp.bfloat16)
    back_rows = lax.psum_scatter(
        spread_rows,
        "seq",
        scatter_dimension=0,
        tiled=True,
    )
    up_grad, down_grad, back_rows = lax.optimization_barrier((up_grad, down_grad, back_rows))
    returned = give_back(back_rows, exp_index, exp_count, mp_count)
    position = my_slice % exp_count
    chosen_by_shift = jnp.take(chosen, (position + jnp.arange(exp_count)) % exp_count, axis=0)
    token_grad = jnp.einsum(
        "kb,krf->brf", chosen_by_shift, returned, preferred_element_type=jnp.float32
    )
    total_grad = output_gradient.astype(jnp.float32) + token_grad.reshape(tokens, slice_width)
    grad_view = total_grad.reshape(tokens, heads_dev, HEAD)
    adjoint = jnp.zeros((heads_dev, HEAD, STATE), jnp.float32)
    back_pieces = [None] * span_count
    for position in reversed(range(span_count)):
        first_row = position * span_rows
        last_row = first_row + span_rows
        cum_block = cum_level[first_row:last_row]
        start_level = cum_level[first_row - 1] if position > 0 else zero_level
        scores = jnp.dot(
            output_state_map[first_row:last_row],
            input_state_map[first_row:last_row].T,
            preferred_element_type=jnp.float32,
        )
        weights = mixing(cum_block, scores, causal)
        weight_high, weight_low = split_parts(weights)
        grad_high, grad_low = split_parts(grad_view[first_row:last_row])
        inner_part = jnp.einsum(
            "hts,thp->shp", weight_high, grad_high, preferred_element_type=jnp.float32
        )
        inner_part = inner_part + jnp.einsum(
            "hts,thp->shp", weight_high, grad_low, preferred_element_type=jnp.float32
        )
        inner_part = inner_part + jnp.einsum(
            "hts,thp->shp", weight_low, grad_high, preferred_element_type=jnp.float32
        )
        end_level = cum_block[-1]
        tail_decay = jnp.exp(end_level[None, :] - cum_block)
        carried = tail_decay[:, :, None] * jnp.einsum(
            "sn,hpn->shp", b_float[first_row:last_row], adjoint, precision=highest
        )
        back_pieces[position] = inner_part + carried
        lead_decay = jnp.exp(cum_block - start_level[None, :])
        adjoint = jnp.exp(end_level - start_level)[:, None, None] * adjoint + jnp.einsum(
            "rhp,rn->hpn",
            grad_view[first_row:last_row] * lead_decay[:, :, None],
            c_float[first_row:last_row],
            precision=highest,
        )
    flat_adjoint = adjoint.reshape(heads_dev, HEAD * STATE)
    adjoint_all = torus_gather(flat_adjoint.astype(jnp.bfloat16), seq_count)
    later_adjoint = carried_sum(adjoint_all, level_all, seq_index, False)
    later_adjoint = later_adjoint.reshape(heads_dev, HEAD, STATE)
    scan_grad = jnp.concatenate(back_pieces, axis=0) + jnp.exp(cum_level[-1][None, :] - cum_level)[
        :, :, None
    ] * jnp.einsum("sn,hpn->shp", b_float, later_adjoint, precision=highest)
    grad_x = total_grad + (input_scale[None, :, None] * scan_grad).reshape(tokens, slice_width)
    return (grad_x, up_grad[None], down_grad[None])


def solution(mesh):
    in_specs = (
        P("seq", ("expert", "mp")),
        P("seq", ("expert", "mp")),
        P("seq", None),
        P("seq", None),
        P(("expert", "mp")),
        P("seq"),
        P(),
        P("expert", "mp", "seq"),
        P("expert", "seq", "mp"),
    )
    out_specs = (P("seq", ("expert", "mp")), P("expert", "mp", "seq"), P("expert", "seq", "mp"))
    return jax.shard_map(
        per_device, mesh=mesh, in_specs=in_specs, out_specs=out_specs, check_vma=False
    )
```

```python
import jax
import jax.numpy as jnp
from jax import lax
from jax.sharding import PartitionSpec as P

HEAD = 64
STATE = 16
BLOCK = 128


spike_position_step = 0.3
highest = lax.Precision.HIGHEST


def carried_sum(values_all, level_all, own, earlier):
    count = level_all.shape[0]
    ids = jnp.arange(count)
    j, k = ids[:, None], ids[None, :]
    if earlier:
        between = (j < k) & (k < own)
        valid = ids < own
    else:
        between = (own < k) & (k < j)
        valid = ids > own
    exponent = jnp.sum(jnp.where(between[:, :, None], level_all[None], 0.0), axis=1)
    weight = jnp.where(valid[:, None], jnp.exp(exponent), 0.0)
    return jnp.sum(weight[:, :, None] * values_all.astype(jnp.float32), axis=0)


def torus_gather(value, count):
    side = 4
    if count != side * side:
        return lax.all_gather(value, "seq")
    own = lax.axis_index("seq")
    row, col = own // side, own % side
    steps = jnp.arange(side)
    got = [value]
    for shift in range(1, side):
        pairs = [(r * side + c, r * side + (c + shift) % side) for r in range(side) for c in range(side)]
        got.append(lax.ppermute(value, "seq", pairs))
    line = jnp.take(jnp.stack(got), (col - steps) % side, axis=0)
    got = [line]
    for shift in range(1, side):
        pairs = [(r * side + c, ((r + shift) % side) * side + c) for r in range(side) for c in range(side)]
        got.append(lax.ppermute(line, "seq", pairs))
    whole = jnp.take(jnp.stack(got), (row - steps) % side, axis=0)
    return whole.reshape((count,) + value.shape)


def mp_sum(part):
    part = part.astype(jnp.bfloat16)
    count = lax.axis_size("mp")
    total = part.astype(jnp.float32)
    for shift in range(1, count):
        pairs = [(src, (src + shift) % count) for src in range(count)]
        total = total + lax.ppermute(part, "mp", pairs).astype(jnp.float32)
    return total


def dispatch_pairs(exp_count, mp_count, shift):
    return [
        (src, ((src % exp_count + shift) % exp_count) * mp_count + src // exp_count)
        for src in range(exp_count * mp_count)
    ]


def dispatch(picks, exp_index, exp_count, mp_count, my_slice):
    position = my_slice % exp_count
    received = []
    for shift in range(exp_count):
        send = lax.dynamic_index_in_dim(picks, (position + shift) % exp_count, 0, keepdims=False)
        pairs = dispatch_pairs(exp_count, mp_count, shift)
        received.append(lax.ppermute(send, ("expert", "mp"), pairs))
    received = jnp.stack(received)
    order = (exp_index - jnp.arange(exp_count)) % exp_count
    placed = jnp.take(received, order, axis=0)
    rows, width = placed.shape[1], placed.shape[2]
    return placed.transpose(1, 0, 2).reshape(rows, exp_count * width)


def give_back(rows_half, exp_index, exp_count, mp_count):
    width = rows_half.shape[1] // exp_count
    pieces = rows_half.reshape(rows_half.shape[0], exp_count, width)
    received = []
    for shift in range(exp_count):
        column = (exp_index - shift) % exp_count
        send = lax.dynamic_index_in_dim(pieces, column, 1, keepdims=False)
        pairs = [(dst, src) for src, dst in dispatch_pairs(exp_count, mp_count, shift)]
        received.append(lax.ppermute(send, ("expert", "mp"), pairs))
    return jnp.stack(received)


def rounded(rounded_in):
    return lax.optimization_barrier(rounded_in.astype(jnp.bfloat16)).astype(jnp.float32)


def split_parts(values):
    high_part = values.astype(jnp.bfloat16)
    low_part = (values - high_part.astype(jnp.float32)).astype(jnp.bfloat16)
    return (high_part, low_part)


def mixing(cum_block, scores, causal):
    spread = cum_block.T[:, :, None] - cum_block.T[:, None, :]
    spread = jnp.where(causal[None], spread, -jnp.inf)
    return jnp.exp(spread) * scores[None]


def compact(select, gathered, half_width):
    blocks = gathered.reshape(select.shape[1], -1, half_width)
    used = jnp.any(select > 0, axis=1)
    source = jnp.argmax(select, axis=1)
    rows_out = jnp.where(used[:, None, None], jnp.take(blocks, source, axis=0, mode="clip"), 0)
    return rows_out.reshape(-1, half_width).astype(jnp.bfloat16)


def spread(present, slot_of, rows, half_width):
    blocks = rows.reshape(-1, BLOCK, half_width)
    placed = jnp.take(blocks, jnp.maximum(slot_of, 0), axis=0, mode="clip")
    placed = jnp.where(present[:, None, None], placed, 0)
    return placed.reshape(-1, half_width).astype(jnp.bfloat16)


def per_device(
    activations,
    output_gradient,
    input_state_map,
    output_state_map,
    head_decay_speed,
    spike_decay_level,
    assign,
    expert_up_weight,
    expert_down_weight,
):
    tokens, slice_width = activations.shape
    heads_dev = slice_width // HEAD
    seq_count = lax.axis_size("seq")
    exp_count = lax.axis_size("expert")
    mp_count = lax.axis_size("mp")
    seq_index = lax.axis_index("seq")
    exp_index = lax.axis_index("expert")
    mp_index = lax.axis_index("mp")
    my_slice = exp_index * mp_count + mp_index
    half_width = slice_width * exp_count
    slot_total = seq_count // 2
    blocks_dev = tokens // BLOCK
    route_table = assign.reshape(seq_count, blocks_dev)
    own_row = lax.dynamic_index_in_dim(route_table, seq_index, 0, keepdims=False)
    chosen = (own_row[None, :] == jnp.arange(exp_count)[:, None]).astype(jnp.bfloat16)
    g_pick = jnp.einsum(
        "eb,brf->erf",
        chosen,
        output_gradient.reshape(blocks_dev, BLOCK, slice_width),
        preferred_element_type=jnp.float32,
    ).astype(jnp.bfloat16)
    g_block = dispatch(g_pick, exp_index, exp_count, mp_count, my_slice)
    g_all = lax.all_gather(g_block, "seq", axis=0)
    present = jnp.any(route_table == exp_index, axis=1)
    slot_of = jnp.cumsum(present.astype(jnp.int32)) - 1
    select = ((slot_of[None, :] == jnp.arange(slot_total)[:, None]) & present[None, :]).astype(
        jnp.bfloat16
    )
    input_scale = jnp.sqrt(1.0 - jnp.exp(-2.0 * head_decay_speed))
    cum_level = jnp.cumsum(
        -head_decay_speed[None, :]
        - spike_position_step * spike_decay_level.astype(jnp.float32)[:, None],
        axis=0,
    )
    b_float = input_state_map.astype(jnp.float32)
    c_float = output_state_map.astype(jnp.float32)
    act_heads = activations.reshape(tokens, heads_dev, HEAD)
    scaled = act_heads.astype(jnp.float32) * input_scale[None, :, None]
    span_rows = min(512, tokens)
    span_count = tokens // span_rows
    causal = jnp.arange(span_rows)[:, None] >= jnp.arange(span_rows)[None, :]
    zero_level = jnp.zeros((heads_dev,), jnp.float32)
    carry_state = jnp.zeros((heads_dev, HEAD, STATE), jnp.float32)
    pieces = []
    for position in range(span_count):
        first_row = position * span_rows
        last_row = first_row + span_rows
        cum_block = cum_level[first_row:last_row]
        start_level = cum_level[first_row - 1] if position > 0 else zero_level
        scores = jnp.dot(
            output_state_map[first_row:last_row],
            input_state_map[first_row:last_row].T,
            preferred_element_type=jnp.float32,
        )
        weights = mixing(cum_block, scores, causal)
        weight_high, weight_low = split_parts(weights)
        x_span = act_heads[first_row:last_row]
        inner_part = jnp.einsum(
            "hts,shp->thp", weight_high, x_span, preferred_element_type=jnp.float32
        )
        inner_part = inner_part + jnp.einsum(
            "hts,shp->thp", weight_low, x_span, preferred_element_type=jnp.float32
        )
        inner_part = inner_part * input_scale[None, :, None]
        carried = jnp.exp(cum_block - start_level[None, :])[:, :, None] * jnp.einsum(
            "tn,hpn->thp", c_float[first_row:last_row], carry_state, precision=highest
        )
        pieces.append(inner_part + carried)
        end_level = cum_block[-1]
        tail_decay = jnp.exp(end_level[None, :] - cum_block)
        carry_state = jnp.exp(end_level - start_level)[:, None, None] * carry_state + jnp.einsum(
            "shp,sn->hpn",
            scaled[first_row:last_row] * tail_decay[:, :, None],
            b_float[first_row:last_row],
            precision=highest,
        )
    flat_state = carry_state.reshape(heads_dev, HEAD * STATE)
    level_lanes = jnp.broadcast_to(cum_level[-1][:, None], (heads_dev, 128))
    joined_all = torus_gather(jnp.concatenate([flat_state, level_lanes], axis=1), seq_count)
    state_all = joined_all[:, :, : HEAD * STATE]
    level_all = joined_all[:, :, HEAD * STATE]
    incoming = carried_sum(state_all, level_all, seq_index, True)
    incoming = incoming.reshape(heads_dev, HEAD, STATE)
    outputs = jnp.concatenate(pieces, axis=0) + jnp.exp(cum_level)[:, :, None] * jnp.einsum(
        "tn,hpn->thp", c_float, incoming, precision=highest
    )
    mixed_out = (activations.astype(jnp.float32) + outputs.reshape(tokens, slice_width)).astype(
        jnp.bfloat16
    )
    g_all, mixed_out = lax.optimization_barrier((g_all, mixed_out))
    h_pick = jnp.einsum(
        "eb,brf->erf",
        chosen,
        mixed_out.reshape(blocks_dev, BLOCK, slice_width),
        preferred_element_type=jnp.float32,
    ).astype(jnp.bfloat16)
    h_block = dispatch(h_pick, exp_index, exp_count, mp_count, my_slice)
    h_all = lax.all_gather(h_block, "seq", axis=0)
    g_rows = compact(select, g_all, half_width)
    down_local = expert_down_weight[0]
    act_grad = mp_sum(
        jnp.einsum("td,fd->tf", g_rows, down_local, preferred_element_type=jnp.float32)
    )
    g_rows, act_grad, h_all = lax.optimization_barrier((g_rows, act_grad, h_all))
    x_rows = compact(select, h_all, half_width)
    up_local = expert_up_weight[0]
    pre_act = mp_sum(jnp.dot(x_rows, up_local, preferred_element_type=jnp.float32))
    activation = jax.nn.silu(pre_act).astype(jnp.bfloat16)
    down_grad = jnp.einsum("tf,td->fd", activation, g_rows, preferred_element_type=jnp.float32)
    sigmoid_pre = jax.nn.sigmoid(pre_act)
    pre_grad = (act_grad * sigmoid_pre * (1.0 + pre_act * (1.0 - sigmoid_pre))).astype(jnp.bfloat16)
    up_grad = jnp.einsum("td,tf->df", x_rows, pre_grad, preferred_element_type=jnp.float32)
    shard_grad = spread(present, slot_of, pre_grad, pre_grad.shape[1])
    row_grad = jnp.einsum("tf,df->td", shard_grad, up_local, preferred_element_type=jnp.float32)
    spread_rows = row_grad.astype(jnp.bfloat16)
    back_rows = lax.psum_scatter(
        spread_rows,
        "seq",
        scatter_dimension=0,
        tiled=True,
    )
    up_grad, down_grad, back_rows = lax.optimization_barrier((up_grad, down_grad, back_rows))
    returned = give_back(back_rows, exp_index, exp_count, mp_count)
    position = my_slice % exp_count
    chosen_by_shift = jnp.take(chosen, (position + jnp.arange(exp_count)) % exp_count, axis=0)
    token_grad = jnp.einsum(
        "kb,krf->brf", chosen_by_shift, returned, preferred_element_type=jnp.float32
    )
    total_grad = output_gradient.astype(jnp.float32) + token_grad.reshape(tokens, slice_width)
    grad_view = total_grad.reshape(tokens, heads_dev, HEAD)
    adjoint = jnp.zeros((heads_dev, HEAD, STATE), jnp.float32)
    back_pieces = [None] * span_count
    for position in reversed(range(span_count)):
        first_row = position * span_rows
        last_row = first_row + span_rows
        cum_block = cum_level[first_row:last_row]
        start_level = cum_level[first_row - 1] if position > 0 else zero_level
        scores = jnp.dot(
            output_state_map[first_row:last_row],
            input_state_map[first_row:last_row].T,
            preferred_element_type=jnp.float32,
        )
        weights = mixing(cum_block, scores, causal)
        weight_high, weight_low = split_parts(weights)
        grad_high, grad_low = split_parts(grad_view[first_row:last_row])
        inner_part = jnp.einsum(
            "hts,thp->shp", weight_high, grad_high, preferred_element_type=jnp.float32
        )
        inner_part = inner_part + jnp.einsum(
            "hts,thp->shp", weight_high, grad_low, preferred_element_type=jnp.float32
        )
        inner_part = inner_part + jnp.einsum(
            "hts,thp->shp", weight_low, grad_high, preferred_element_type=jnp.float32
        )
        end_level = cum_block[-1]
        tail_decay = jnp.exp(end_level[None, :] - cum_block)
        carried = tail_decay[:, :, None] * jnp.einsum(
            "sn,hpn->shp", b_float[first_row:last_row], adjoint, precision=highest
        )
        back_pieces[position] = inner_part + carried
        lead_decay = jnp.exp(cum_block - start_level[None, :])
        adjoint = jnp.exp(end_level - start_level)[:, None, None] * adjoint + jnp.einsum(
            "rhp,rn->hpn",
            grad_view[first_row:last_row] * lead_decay[:, :, None],
            c_float[first_row:last_row],
            precision=highest,
        )
    flat_adjoint = adjoint.reshape(heads_dev, HEAD * STATE)
    adjoint_all = torus_gather(flat_adjoint.astype(jnp.bfloat16), seq_count)
    later_adjoint = carried_sum(adjoint_all, level_all, seq_index, False)
    later_adjoint = later_adjoint.reshape(heads_dev, HEAD, STATE)
    scan_grad = jnp.concatenate(back_pieces, axis=0) + jnp.exp(cum_level[-1][None, :] - cum_level)[
        :, :, None
    ] * jnp.einsum("sn,hpn->shp", b_float, later_adjoint, precision=highest)
    grad_x = total_grad + (input_scale[None, :, None] * scan_grad).reshape(tokens, slice_width)
    return (grad_x, up_grad[None], down_grad[None])


def solution(mesh):
    in_specs = (
        P("seq", ("expert", "mp")),
        P("seq", ("expert", "mp")),
        P("seq", None),
        P("seq", None),
        P(("expert", "mp")),
        P("seq"),
        P(),
        P("expert", "mp", "seq"),
        P("expert", "seq", "mp"),
    )
    out_specs = (P("seq", ("expert", "mp")), P("expert", "mp", "seq"), P("expert", "seq", "mp"))
    return jax.shard_map(
        per_device, mesh=mesh, in_specs=in_specs, out_specs=out_specs, check_vma=False
    )
```
